256 devices in a mesh: sec: 2 (over y_lo), dp: 8 (over x, y_hi), seq: 16 (over z, core).
Axes of the slice: x: 4, y: 4 (y_hi: 2, y_lo: 2; y = y_hi * 2 + y_lo), z: 8, core: 2. Of those that a mesh axis runs over, the one named last changes fastest.
Arguments:
- hidden: bfloat16 [256, 128, 2560], P(('sec', 'dp', 'seq')), may hold values from -24 to 24
- cond_shift: bfloat16 [256, 2560], P(('sec', 'dp', 'seq')), may hold values from -0.3125 to 0.3125
- cond_scale: bfloat16 [256, 2560], P(('sec', 'dp', 'seq')), may hold values from -1.75 to 1.75
- noisy: bfloat16 [256, 128, 256], P(('sec', 'dp', 'seq')), may hold values from -6 to 6
- noise_level: float32 [256], P(('sec', 'dp', 'seq')), may hold values from 0.2 to 1
- w_out: bfloat16 [2560, 256], replicated, may hold values from -0.125 to 0.125
- w_embed: bfloat16 [256, 2048], replicated, may hold values from -0.375 to 0.375
- w_root: bfloat16 [2, 2048], replicated, may hold values from -0.03125 to 0.03125
- w_qkv: bfloat16 [3, 2048, 2048], P(None, None, 'seq'), may hold values from -0.125 to 0.125
- w_proj: bfloat16 [2048, 512], P('seq'), may hold values from -0.125 to 0.125
- text_table: bfloat16 [49408, 512], P('seq'), may hold values from -6 to 6
- text_ids: int32 [32, 32], replicated, may hold values from 0 to 49407
- prompt_index: int32 [256], P(('sec', 'dp')), may hold values from 0 to 31
- reward_weight: float32 [256], P(('sec', 'dp')), may hold values from 1000 to 4000
Outputs:
- rewards: float32 [256], P(('sec', 'dp'))
- grad_w_out: float32 [2560, 256], P('seq')
- grad_hidden: bfloat16 [256, 128, 2560], P(('sec', 'dp', 'seq'))
The draws below stay inside these ranges and needn't reach their ends.
All inputs are finite; a program needn't handle non-finite values.
Results may differ from the reference program's by a relative error of at most 0.017.
The reference program's roundings to bfloat16 on the way count: a program that leaves them out, or rounds other values in their place, can miss the bound.
Values may be sent and summed in bfloat16 or wider, within the bound.
No kernel may reach another device: no remote copies, remote signals or barrier semaphores. Data moves between devices by JAX's collectives and lax.ppermute only.
A program may use at most 128 MiB of HBM per device.

```python
import math
import jax
import jax.numpy as jnp
import numpy as np
from jax import lax

D_GEN = 2560
D_REW = 2048
HEADS = 16
FEAT = 256
EMBED = 512
VOCAB = 49408
FRAMES = 128
PROMPTS = 32
TEXT_LEN = 32
CLIPS = 256


def touch_ends(result, rng, smallest, largest):
    place = [jax.random.randint(jax.random.fold_in(rng, axis), (), 0, length) for axis, length in enumerate(result.shape)]
    main_axis = result.shape.index(max(result.shape))
    next_to = place[:main_axis] + [(place[main_axis] + 1) % result.shape[main_axis]] + place[main_axis + 1:]
    return result.at[tuple(place)].set(smallest).at[tuple(next_to)].set(largest)


def raised(entries, key, source, target, shards_of, factor):
    owner, partner = [(jnp.arange(entries.shape[axis_at]) // (entries.shape[axis_at] // shards_of)).reshape([-1 if axis == axis_at else 1 for axis in range(entries.ndim)]) for axis_at in (source, target)]
    chosen = jax.random.permutation(key, shards_of)[partner]
    strong = (owner == chosen) | (owner == (partner + shards_of // 2) % shards_of)
    return jnp.where(strong, factor * entries, entries)


def block_levels(stream_key, dims, cuts, least, high):
    level, own = 1.0, jax.random.fold_in(stream_key, 6)
    for position, shards_of in cuts:
        steps = jnp.exp(jax.random.uniform(jax.random.fold_in(own, position), (shards_of,), jnp.float32, least / len(cuts), high / len(cuts)))
        level = level * jnp.repeat(steps, dims[position] // shards_of).reshape([-1 if axis == position else 1 for axis in range(len(dims))])
    return level


def rank_table(count, skew):
    weights = [(1 << 20) // math.isqrt(rank ** skew) + 1 for rank in range(1, count + 1)]
    deviation = 1 + sum(weights) // (1 << 30)
    return np.cumsum(np.array([max(1, weight // deviation) for weight in weights]))


def ranked_ids(stream_key, dims, number_of, lean):
    grid = rank_table(number_of, lean)
    pick = jax.random.randint(jax.random.fold_in(stream_key, 1), dims, 0, int(grid[number_of - 1]))
    grade = jnp.searchsorted(jnp.asarray(grid, jnp.int32), pick, side="right")
    return jax.random.permutation(jax.random.fold_in(stream_key, 2), number_of)[grade].astype(jnp.int32)


def gaussian(rng, shape, width, most, split=(), kind=jnp.bfloat16):
    array = width * jax.random.normal(rng, shape, jnp.float32)
    if split:
        array = array * block_levels(rng, shape, split, -0.22, 0.18)
    return jnp.clip(array, -most, most).astype(kind)


def heavy_noise(key, shape, spread, bound, shards, heavy, dtype=jnp.bfloat16):
    array = spread * jax.random.normal(key, shape, jnp.float32)
    if shards:
        array = array * block_levels(key, shape, shards, -0.22, 0.18)
    return jnp.clip(raised(array, jax.random.fold_in(key, 3), *heavy), -bound, bound).astype(dtype)


def setup_inputs(seed: int = 0) -> dict:
    arg_keys = jax.random.split(jax.random.key(seed), 15)
    hidden = heavy_noise(arg_keys[0], (CLIPS, FRAMES, D_GEN), 1.0, 24.0, ((0, 256),), (0, 2, 256, 6.0))
    cond_shift = gaussian(arg_keys[1], (CLIPS, D_GEN), 0.05, 0.3125, ((0, 256),))
    cond_scale = gaussian(arg_keys[2], (CLIPS, D_GEN), 0.3, 1.75, ((0, 256),))
    noisy = gaussian(arg_keys[3], (CLIPS, FRAMES, FEAT), 1.0, 6.0, ((0, 256),))
    noise_level = jnp.clip(jnp.exp(math.log(1.0) - 1.609438 * jax.random.uniform(arg_keys[4], (CLIPS,), jnp.float32) ** block_levels(arg_keys[4], (CLIPS,), ((0, 256),), -0.2, 0.2)), 0.2, 1.0)
    w_out = gaussian(arg_keys[5], (D_GEN, FEAT), D_GEN ** -0.5, 0.125)
    w_embed = gaussian(arg_keys[6], (FEAT, D_REW), FEAT ** -0.5, 0.375)
    w_root = gaussian(arg_keys[7], (2, D_REW), 0.005, 0.03125)
    w_qkv = gaussian(arg_keys[8], (3, D_REW, D_REW), D_REW ** -0.5, 0.125, ((2, 16),))
    w_proj = gaussian(arg_keys[9], (D_REW, EMBED), D_REW ** -0.5, 0.125, ((0, 16),))
    text_table = gaussian(arg_keys[10], (VOCAB, EMBED), 1.0, 6.0, ((0, 16),))
    text_ids = touch_ends(ranked_ids(arg_keys[11], (PROMPTS, TEXT_LEN), VOCAB, 2), jax.random.fold_in(arg_keys[11], 3), 0, VOCAB - 1).astype(jnp.int32)
    prompt_index = touch_ends(jax.random.randint(arg_keys[12], (CLIPS,), 0, PROMPTS), jax.random.fold_in(arg_keys[12], 1), 0, PROMPTS - 1).astype(jnp.int32)
    reward_weight = jnp.clip(1000.0 + 3000.0 * jax.random.uniform(arg_keys[13], (CLIPS,), jnp.float32) ** block_levels(arg_keys[13], (CLIPS,), ((0, 16),), -0.2, 0.2), 1000.0, 4000.0)
    return dict(hidden=hidden, cond_shift=cond_shift, cond_scale=cond_scale, noisy=noisy, noise_level=noise_level, w_out=w_out, w_embed=w_embed, w_root=w_root, w_qkv=w_qkv, w_proj=w_proj, text_table=text_table, text_ids=text_ids, prompt_index=prompt_index, reward_weight=reward_weight)


normalizing_sharpness = 10.0
epsilon = 1e-06
highest = lax.Precision.HIGHEST

def rotate(angle, first, second):
    cosine = jnp.cos(angle)
    sine_term = jnp.sin(angle)
    return (cosine * first + sine_term * second, cosine * second - sine_term * first)

def suffix(values):
    return lax.optimization_barrier(jnp.sum(values, axis=0, keepdims=True)) - jnp.cumsum(values, axis=0)

def unit_rows(vectors):
    length = jnp.sqrt(lax.optimization_barrier(jnp.sum(vectors * vectors, axis=-1, keepdims=True)) + epsilon)
    return (vectors / length, length)

def reference(hidden, cond_shift, cond_scale, noisy, noise_level, w_out, w_embed, w_root, w_qkv, w_proj, text_table, text_ids, prompt_index, reward_weight):
    head_size = D_REW // HEADS
    root_rows = w_root.astype(jnp.float32)
    embed_rows = w_embed.astype(jnp.float32)
    proj_rows = w_proj.astype(jnp.float32)
    text_raw = lax.optimization_barrier(jnp.sum(text_table[text_ids].astype(jnp.float32), axis=1))
    text_unit, text_len = unit_rows(text_raw)

    def one_clip(total, item):
        clip_hidden, shift_row, scale_row, clip_noisy, level, prompt, weight = item
        hidden_f = clip_hidden.astype(jnp.float32)
        centred = hidden_f - lax.optimization_barrier(jnp.mean(hidden_f, axis=-1, keepdims=True))
        inv_std = lax.rsqrt(lax.optimization_barrier(jnp.mean(centred * centred, axis=-1, keepdims=True)) + epsilon)
        normed_h = centred * inv_std
        gain = 1.0 + scale_row.astype(jnp.float32)[None, :]
        modulated = (normed_h * gain + shift_row.astype(jnp.float32)[None, :]).astype(jnp.bfloat16)
        eps_pred = jnp.dot(modulated, w_out, preferred_element_type=jnp.float32)
        x_clean = clip_noisy.astype(jnp.float32) - level * eps_pred
        spin = x_clean[:, 0]
        theta = jnp.cumsum(spin) - spin
        step_east, step_north = rotate(theta, x_clean[:, 1], x_clean[:, 2])
        root_east = jnp.cumsum(step_east) - step_east
        root_north = jnp.cumsum(step_north) - step_north
        emb = jnp.dot(x_clean.astype(jnp.bfloat16), w_embed, preferred_element_type=jnp.float32)
        emb = emb + root_east[:, None] * root_rows[0] + root_north[:, None] * root_rows[1]
        scale_rms = jnp.sqrt(lax.optimization_barrier(jnp.mean(emb * emb, axis=-1, keepdims=True)) + epsilon)
        normed_e = emb / scale_rms
        emb_b = normed_e.astype(jnp.bfloat16)
        query = jnp.dot(emb_b, w_qkv[0], preferred_element_type=jnp.float32).reshape(FRAMES, HEADS, head_size)
        keys = jnp.dot(emb_b, w_qkv[1], preferred_element_type=jnp.float32).reshape(FRAMES, HEADS, head_size)
        values = jnp.dot(emb_b, w_qkv[2], preferred_element_type=jnp.float32).reshape(FRAMES, HEADS, head_size)
        query_unit, query_len = unit_rows(query)
        key_unit, key_len = unit_rows(keys)
        asking_vectors_group = query_unit.astype(jnp.bfloat16)
        lookup_vectors_group = key_unit.astype(jnp.bfloat16)
        value_b = values.astype(jnp.bfloat16)
        similarity_table = normalizing_sharpness * jnp.einsum('fnl,xnl->nfx', asking_vectors_group.astype(jnp.float32), lookup_vectors_group.astype(jnp.float32))
        expo = jnp.exp(similarity_table)
        focus_probabilities = expo / lax.optimization_barrier(jnp.sum(expo, axis=-1, keepdims=True))
        attention_b = focus_probabilities.astype(jnp.bfloat16)
        column_mass = lax.optimization_barrier(jnp.sum(attention_b.astype(jnp.float32), axis=1))
        value_f = value_b.astype(jnp.float32)
        pooled = jnp.einsum('hg,ghd->hd', column_mass, value_f, precision=highest)
        pooled_b = pooled.astype(jnp.bfloat16).reshape(1, D_REW)
        motion_emb = jnp.dot(pooled_b, w_proj, preferred_element_type=jnp.float32)[0]
        target = text_unit[prompt]
        emb_len = jnp.sqrt(jnp.sum(motion_emb * motion_emb) + epsilon)
        reward = jnp.sum(motion_emb * target) / emb_len
        d_memb = -weight * (target - reward * motion_emb / emb_len) / emb_len
        d_pooled = jnp.dot(d_memb[None, :], proj_rows.T, precision=highest)[0].reshape(HEADS, head_size)
        reduction_dimension = jnp.einsum('hd,ghd->hg', d_pooled, value_f, precision=highest)
        d_value = jnp.transpose(column_mass, (1, 0))[:, :, None] * d_pooled[None, :, :]
        pairwise_dot_similarity = lax.optimization_barrier(jnp.sum(focus_probabilities * reduction_dimension[:, None, :], axis=-1, keepdims=True))
        similarity_derivative = (normalizing_sharpness * focus_probabilities * (reduction_dimension[:, None, :] - pairwise_dot_similarity)).astype(jnp.bfloat16)
        d_qu = jnp.einsum('hfg,ghd->fhd', similarity_derivative.astype(jnp.float32), lookup_vectors_group.astype(jnp.float32))
        d_ku = jnp.einsum('hfg,fhd->ghd', similarity_derivative.astype(jnp.float32), asking_vectors_group.astype(jnp.float32))
        d_query = (d_qu - query_unit * lax.optimization_barrier(jnp.sum(query_unit * d_qu, axis=-1, keepdims=True))) / query_len
        d_key = (d_ku - key_unit * lax.optimization_barrier(jnp.sum(key_unit * d_ku, axis=-1, keepdims=True))) / key_len
        d_emb = jnp.dot(d_query.astype(jnp.bfloat16).reshape(FRAMES, D_REW), w_qkv[0].T, preferred_element_type=jnp.float32)
        d_emb = d_emb + jnp.dot(d_key.astype(jnp.bfloat16).reshape(FRAMES, D_REW), w_qkv[1].T, preferred_element_type=jnp.float32)
        d_emb = d_emb + jnp.dot(d_value.astype(jnp.bfloat16).reshape(FRAMES, D_REW), w_qkv[2].T, preferred_element_type=jnp.float32)
        d_unemb = (d_emb - normed_e * lax.optimization_barrier(jnp.mean(d_emb * normed_e, axis=-1, keepdims=True))) / scale_rms
        d_clean = jnp.dot(d_unemb, embed_rows.T, precision=highest)
        grad_east = suffix(lax.optimization_barrier(jnp.sum(d_unemb * root_rows[0], axis=-1)))
        grad_north = suffix(lax.optimization_barrier(jnp.sum(d_unemb * root_rows[1], axis=-1)))
        d_east, d_north = rotate(-theta, grad_east, grad_north)
        cosine = jnp.cos(theta)
        sine_term = jnp.sin(theta)
        vel_east = x_clean[:, 1]
        vel_north = x_clean[:, 2]
        d_theta = grad_east * (cosine * vel_north - sine_term * vel_east) - grad_north * (cosine * vel_east + sine_term * vel_north)
        d_spin = suffix(d_theta)
        d_clean = d_clean.at[:, 0].add(d_spin).at[:, 1].add(d_east).at[:, 2].add(d_north)
        d_eps_b = (-level * d_clean).astype(jnp.bfloat16)
        grad_term = jnp.dot(modulated.T, d_eps_b, preferred_element_type=jnp.float32)
        d_mod = jnp.dot(d_eps_b, w_out.T, preferred_element_type=jnp.float32)
        d_norm = d_mod * gain
        grad_clip = (inv_std * (d_norm - lax.optimization_barrier(jnp.mean(d_norm, axis=-1, keepdims=True)) - normed_h * lax.optimization_barrier(jnp.mean(d_norm * normed_h, axis=-1, keepdims=True)))).astype(jnp.bfloat16)
        return (total + grad_term, (reward, grad_clip))
    start_total = jnp.zeros((D_GEN, FEAT), jnp.float32)
    total, outputs = lax.scan(one_clip, start_total, (hidden, cond_shift, cond_scale, noisy, noise_level, prompt_index, reward_weight))
    return (outputs[0], total, outputs[1])
```

```python
import jax
import jax.numpy as jnp
from jax import lax
from jax.sharding import PartitionSpec as P

D_REW = 2048
HEADS = 16
PROMPTS = 32


normalizing_sharpness = 10.0
epsilon = 1e-06
highest = lax.Precision.HIGHEST


def rotate(angle, first, second):
    cosine = jnp.cos(angle)
    sine_term = jnp.sin(angle)
    return (cosine * first + sine_term * second, cosine * second - sine_term * first)


def suffix(values):
    return jnp.sum(values, axis=1, keepdims=True) - jnp.cumsum(values, axis=1)


def local_path(motion):
    spin = motion[..., 0]
    theta = jnp.cumsum(spin, axis=1) - spin
    step_east, step_north = rotate(theta, motion[..., 1], motion[..., 2])
    path_east = jnp.cumsum(step_east, axis=1) - step_east
    path_north = jnp.cumsum(step_north, axis=1) - step_north
    return (theta, path_east, path_north)


def embed(motion, root_east, root_north, w_embed, root_rows):
    emb = jnp.einsum(
        "cfe,ed->cfd", motion.astype(jnp.bfloat16), w_embed, preferred_element_type=jnp.float32
    )
    emb = emb + root_east[..., None] * root_rows[0] + root_north[..., None] * root_rows[1]
    scale_rms = jnp.sqrt(jnp.mean(emb * emb, axis=-1, keepdims=True) + epsilon)
    return (emb / scale_rms, scale_rms)


def unit_rows(vectors):
    length = jnp.sqrt(jnp.sum(vectors * vectors, axis=-1, keepdims=True) + epsilon)
    return (vectors / length, length)


def norm_grad(grad, normed, scale_rms):
    return (grad - normed * jnp.mean(grad * normed, axis=-1, keepdims=True)) / scale_rms


def motion_grad(d_emb, normed_e, scale_rms, motion, theta, embed_rows, root_rows):
    d_unemb = norm_grad(d_emb, normed_e, scale_rms)
    d_embedded = jnp.einsum("cfd,ed->cfe", d_unemb, embed_rows, precision=highest)
    grad_east = suffix(jnp.sum(d_unemb * root_rows[0], axis=-1))
    grad_north = suffix(jnp.sum(d_unemb * root_rows[1], axis=-1))
    vel_east = motion[..., 1]
    vel_north = motion[..., 2]
    d_east, d_north = rotate(-theta, grad_east, grad_north)
    cosine = jnp.cos(theta)
    sine_term = jnp.sin(theta)
    d_theta = grad_east * (cosine * vel_north - sine_term * vel_east) - grad_north * (
        cosine * vel_east + sine_term * vel_north
    )
    d_spin = suffix(d_theta)
    return d_embedded.at[..., 0].add(d_spin).at[..., 1].add(d_east).at[..., 2].add(d_north)


def local(
    hidden,
    cond_shift,
    cond_scale,
    noisy,
    noise_level,
    w_out,
    w_embed,
    w_root,
    w_qkv,
    w_proj,
    text_table,
    text_ids,
    prompt_index,
    reward_weight,
):
    clips_dev = hidden.shape[0]
    ways = lax.axis_size("seq")
    me = lax.axis_index("seq")
    head_size = D_REW // HEADS
    root_rows = w_root.astype(jnp.float32)
    embed_rows = w_embed.astype(jnp.float32)

    vocab_rows = text_table.shape[0]
    local_ids = text_ids - me * vocab_rows
    inside = (local_ids >= 0) & (local_ids < vocab_rows)
    picked = jnp.take(text_table, jnp.clip(local_ids, 0, vocab_rows - 1), axis=0).astype(
        jnp.float32
    )
    text_part = jnp.sum(jnp.where(inside[..., None], picked, 0.0), axis=1)
    proj_dev = w_proj.shape[0]
    proj_text = lax.all_gather(
        jnp.concatenate([w_proj.astype(jnp.float32), text_part], axis=0), "seq", axis=0
    )
    proj_rows = proj_text[:, :proj_dev].reshape(ways * proj_dev, w_proj.shape[1])
    text_raw = jnp.sum(proj_text[:, proj_dev:], axis=0)
    text_unit, text_len = unit_rows(text_raw)

    w_all = lax.all_gather(w_qkv, "seq", axis=0)

    hidden_f = hidden.astype(jnp.float32)
    centred = hidden_f - jnp.mean(hidden_f, axis=-1, keepdims=True)
    inv_std = lax.rsqrt(jnp.mean(centred * centred, axis=-1, keepdims=True) + epsilon)
    normed_h = centred * inv_std
    gain = 1.0 + cond_scale.astype(jnp.float32)[:, None, :]
    modulated = (normed_h * gain + cond_shift.astype(jnp.float32)[:, None, :]).astype(jnp.bfloat16)
    eps_pred = jnp.einsum("cfd,de->cfe", modulated, w_out, preferred_element_type=jnp.float32)
    level = noise_level[:, None, None]
    x_clean = noisy.astype(jnp.float32) - level * eps_pred
    theta, path_east, path_north = local_path(x_clean)
    normed_e, scale_rms = embed(x_clean, path_east, path_north, w_embed, root_rows)
    projected = jnp.einsum(
        "cfd,hjdk->cfhjk",
        normed_e.astype(jnp.bfloat16),
        w_all,
        preferred_element_type=jnp.float32,
    )
    query_unit, query_len = unit_rows(projected[:, :, :, 0])
    key_unit, key_len = unit_rows(projected[:, :, :, 1])
    asking_vectors_group = query_unit.astype(jnp.bfloat16)
    lookup_vectors_group = key_unit.astype(jnp.bfloat16)
    value_b = projected[:, :, :, 2].astype(jnp.bfloat16)
    similarity_table = normalizing_sharpness * jnp.einsum(
        "cfhd,cghd->chfg",
        asking_vectors_group,
        lookup_vectors_group,
        preferred_element_type=jnp.float32,
    )
    expo = jnp.exp(similarity_table)
    focus_probabilities = expo / jnp.sum(expo, axis=-1, keepdims=True)
    attention_b = focus_probabilities.astype(jnp.bfloat16)
    column_mass = jnp.sum(attention_b, axis=2, dtype=jnp.float32)
    value_f = value_b.astype(jnp.float32)
    pooled = jnp.einsum("chg,cghd->chd", column_mass, value_f, precision=highest)
    pooled_b = pooled.astype(jnp.bfloat16).reshape(clips_dev, D_REW)
    motion_emb = jnp.dot(
        pooled_b, proj_rows.astype(jnp.bfloat16), preferred_element_type=jnp.float32
    )
    prompts = lax.dynamic_slice_in_dim(prompt_index, me * clips_dev, clips_dev)
    weights = lax.dynamic_slice_in_dim(reward_weight, me * clips_dev, clips_dev)
    choose = (prompts[:, None] == jnp.arange(PROMPTS)[None, :]).astype(jnp.float32)
    target = jnp.dot(choose, text_unit, precision=highest)
    emb_len = jnp.sqrt(jnp.sum(motion_emb * motion_emb, axis=-1) + epsilon)
    rewards = jnp.sum(motion_emb * target, axis=-1) / emb_len
    d_memb = (
        (-weights)[:, None]
        * (target - rewards[:, None] * motion_emb / emb_len[:, None])
        / emb_len[:, None]
    )
    d_pooled = jnp.dot(d_memb, proj_rows.T, precision=highest).reshape(
        clips_dev, HEADS, head_size
    )
    reduction_dimension = jnp.einsum("chd,cghd->chg", d_pooled, value_f, precision=highest)
    d_value = jnp.transpose(column_mass, (0, 2, 1))[..., None] * d_pooled[:, None]
    pairwise_dot_similarity = jnp.sum(
        focus_probabilities * reduction_dimension[:, :, None, :], axis=-1, keepdims=True
    )
    similarity_derivative = (
        normalizing_sharpness
        * focus_probabilities
        * (reduction_dimension[:, :, None, :] - pairwise_dot_similarity)
    ).astype(jnp.bfloat16)
    d_qu = jnp.einsum(
        "chfg,cghd->cfhd",
        similarity_derivative,
        lookup_vectors_group,
        preferred_element_type=jnp.float32,
    )
    d_ku = jnp.einsum(
        "chfg,cfhd->cghd",
        similarity_derivative,
        asking_vectors_group,
        preferred_element_type=jnp.float32,
    )
    d_query = (d_qu - query_unit * jnp.sum(query_unit * d_qu, axis=-1, keepdims=True)) / query_len
    d_key = (d_ku - key_unit * jnp.sum(key_unit * d_ku, axis=-1, keepdims=True)) / key_len
    d_proj = jnp.stack([d_query, d_key, d_value], axis=3).astype(jnp.bfloat16)
    d_emb = jnp.einsum("cfhjk,hjdk->cfd", d_proj, w_all, preferred_element_type=jnp.float32)
    d_motion = motion_grad(d_emb, normed_e, scale_rms, x_clean, theta, embed_rows, root_rows)
    d_eps_b = (-level * d_motion).astype(jnp.bfloat16)
    d_mod = jnp.einsum("cfe,de->cfd", d_eps_b, w_out, preferred_element_type=jnp.float32)
    d_norm = d_mod * gain
    grad_hidden = (
        inv_std
        * (
            d_norm
            - jnp.mean(d_norm, axis=-1, keepdims=True)
            - normed_h * jnp.mean(d_norm * normed_h, axis=-1, keepdims=True)
        )
    ).astype(jnp.bfloat16)
    grad_term = jnp.einsum("cfd,cfe->de", modulated, d_eps_b, preferred_element_type=jnp.float32)

    rows_dev = w_out.shape[0] // ways
    cols = grad_term.shape[1]
    n_dp = lax.axis_size("dp")
    total_clips = clips_dev * ways * n_dp * lax.axis_size("sec")
    extra = -(-total_clips // cols)
    extra = -(-extra // 8) * 8
    first_clip = (
        (lax.axis_index("sec") * n_dp + lax.axis_index("dp")) * ways + me
    ) * clips_dev
    columns = jnp.arange(extra * cols)
    slots = columns[None, :] == (first_clip + jnp.arange(clips_dev))[:, None]
    reward_rows = jnp.sum(jnp.where(slots, rewards[:, None], 0.0), axis=0).reshape(extra, cols)
    stacked = jnp.concatenate(
        [
            grad_term.reshape(ways, rows_dev, cols),
            jnp.broadcast_to(reward_rows[None], (ways, extra, cols)),
        ],
        axis=1,
    ).reshape(ways * (rows_dev + extra), cols)
    block = lax.psum_scatter(stacked, "seq", scatter_dimension=0, tiled=True)
    block = lax.psum(block, ("sec", "dp"))
    grad_w_out = block[:rows_dev]
    group_first = (lax.axis_index("sec") * n_dp + lax.axis_index("dp")) * ways * clips_dev
    all_rewards = block[rows_dev:].reshape(extra * cols)
    rewards_out = lax.dynamic_slice_in_dim(all_rewards, group_first, ways * clips_dev)
    return (rewards_out, grad_w_out, grad_hidden)


def solution(mesh):
    placed = (
        P(("sec", "dp", "seq"), None, None),
        P(("sec", "dp", "seq"), None),
        P(("sec", "dp", "seq"), None),
        P(("sec", "dp", "seq"), None, None),
        P(("sec", "dp", "seq")),
        P(),
        P(),
        P(),
        P(None, None, "seq"),
        P("seq", None),
        P("seq", None),
        P(),
        P(("sec", "dp")),
        P(("sec", "dp")),
    )
    return jax.shard_map(
        local,
        mesh=mesh,
        in_specs=placed,
        out_specs=(P(("sec", "dp")), P("seq", None), P(("sec", "dp", "seq"), None, None)),
        check_vma=False,
    )
```

```python
import jax
import jax.numpy as jnp
from jax import lax
from jax.sharding import PartitionSpec as P

D_REW = 2048
HEADS = 16
PROMPTS = 32


normalizing_sharpness = 10.0
epsilon = 1e-06
highest = lax.Precision.HIGHEST


def rotate(angle, first, second):
    cosine = jnp.cos(angle)
    sine_term = jnp.sin(angle)
    return (cosine * first + sine_term * second, cosine * second - sine_term * first)


def suffix(values):
    return jnp.sum(values, axis=1, keepdims=True) - jnp.cumsum(values, axis=1)


def local_path(motion):
    spin = motion[..., 0]
    theta = jnp.cumsum(spin, axis=1) - spin
    step_east, step_north = rotate(theta, motion[..., 1], motion[..., 2])
    path_east = jnp.cumsum(step_east, axis=1) - step_east
    path_north = jnp.cumsum(step_north, axis=1) - step_north
    return (theta, path_east, path_north)


def embed(motion, root_east, root_north, w_embed, root_rows):
    emb = jnp.einsum(
        "cfe,ed->cfd", motion.astype(jnp.bfloat16), w_embed, preferred_element_type=jnp.float32
    )
    emb = emb + root_east[..., None] * root_rows[0] + root_north[..., None] * root_rows[1]
    scale_rms = jnp.sqrt(jnp.mean(emb * emb, axis=-1, keepdims=True) + epsilon)
    return (emb / scale_rms, scale_rms)


def unit_rows(vectors):
    length = jnp.sqrt(jnp.sum(vectors * vectors, axis=-1, keepdims=True) + epsilon)
    return (vectors / length, length)


def norm_grad(grad, normed, scale_rms):
    return (grad - normed * jnp.mean(grad * normed, axis=-1, keepdims=True)) / scale_rms


def motion_grad(d_emb, normed_e, scale_rms, motion, theta, embed_rows, root_rows):
    d_unemb = norm_grad(d_emb, normed_e, scale_rms)
    d_embedded = jnp.einsum("cfd,ed->cfe", d_unemb, embed_rows, precision=highest)
    grad_east = suffix(jnp.sum(d_unemb * root_rows[0], axis=-1))
    grad_north = suffix(jnp.sum(d_unemb * root_rows[1], axis=-1))
    vel_east = motion[..., 1]
    vel_north = motion[..., 2]
    d_east, d_north = rotate(-theta, grad_east, grad_north)
    cosine = jnp.cos(theta)
    sine_term = jnp.sin(theta)
    d_theta = grad_east * (cosine * vel_north - sine_term * vel_east) - grad_north * (
        cosine * vel_east + sine_term * vel_north
    )
    d_spin = suffix(d_theta)
    return d_embedded.at[..., 0].add(d_spin).at[..., 1].add(d_east).at[..., 2].add(d_north)


def xor_pairs(size, bit):
    return [(i, i ^ bit) for i in range(size)]


def halving_sum(chunks, axis):
    size = lax.axis_size(axis)
    me = lax.axis_index(axis)
    bits = size.bit_length() - 1
    assert 1 << bits == size
    buf = chunks.reshape((2,) * bits + chunks.shape[1:])
    for k in range(bits):
        mine = (me >> k) & 1
        keep = lax.dynamic_index_in_dim(buf, mine, axis=bits - 1 - k, keepdims=False)
        send = lax.dynamic_index_in_dim(buf, 1 - mine, axis=bits - 1 - k, keepdims=False)
        buf = keep + lax.ppermute(send, axis, xor_pairs(size, 1 << k))
    return buf


def doubling_sum(value, axis):
    size = lax.axis_size(axis)
    bits = size.bit_length() - 1
    assert 1 << bits == size
    for k in range(bits):
        value = value + lax.ppermute(value, axis, xor_pairs(size, 1 << k))
    return value


def local(
    hidden,
    cond_shift,
    cond_scale,
    noisy,
    noise_level,
    w_out,
    w_embed,
    w_root,
    w_qkv,
    w_proj,
    text_table,
    text_ids,
    prompt_index,
    reward_weight,
):
    clips_dev = hidden.shape[0]
    ways = lax.axis_size("seq")
    me = lax.axis_index("seq")
    head_size = D_REW // HEADS
    root_rows = w_root.astype(jnp.float32)
    embed_rows = w_embed.astype(jnp.float32)

    vocab_rows = text_table.shape[0]
    local_ids = text_ids - me * vocab_rows
    inside = (local_ids >= 0) & (local_ids < vocab_rows)
    picked = jnp.take(text_table, jnp.clip(local_ids, 0, vocab_rows - 1), axis=0).astype(
        jnp.float32
    )
    text_part = jnp.sum(jnp.where(inside[..., None], picked, 0.0), axis=1)
    w_all = lax.all_gather(w_qkv, "seq", axis=0)

    hidden_f = hidden.astype(jnp.float32)
    centred = hidden_f - jnp.mean(hidden_f, axis=-1, keepdims=True)
    inv_std = lax.rsqrt(jnp.mean(centred * centred, axis=-1, keepdims=True) + epsilon)
    normed_h = centred * inv_std
    gain = 1.0 + cond_scale.astype(jnp.float32)[:, None, :]
    modulated = (normed_h * gain + cond_shift.astype(jnp.float32)[:, None, :]).astype(jnp.bfloat16)
    eps_pred = jnp.einsum("cfd,de->cfe", modulated, w_out, preferred_element_type=jnp.float32)
    level = noise_level[:, None, None]
    x_clean = noisy.astype(jnp.float32) - level * eps_pred
    theta, path_east, path_north = local_path(x_clean)
    normed_e, scale_rms = embed(x_clean, path_east, path_north, w_embed, root_rows)
    proj_dev = w_proj.shape[0]
    w_all, proj_send, emb_b = lax.optimization_barrier(
        (
            w_all,
            jnp.concatenate([w_proj.astype(jnp.float32), text_part], axis=0),
            normed_e.astype(jnp.bfloat16),
        )
    )
    proj_text = lax.all_gather(proj_send, "seq", axis=0)
    proj_rows = proj_text[:, :proj_dev].reshape(ways * proj_dev, w_proj.shape[1])
    text_raw = jnp.sum(proj_text[:, proj_dev:], axis=0)
    text_unit, text_len = unit_rows(text_raw)
    projected = jnp.einsum(
        "cfd,hjdk->cfhjk",
        emb_b,
        w_all,
        preferred_element_type=jnp.float32,
    )
    query_unit, query_len = unit_rows(projected[:, :, :, 0])
    key_unit, key_len = unit_rows(projected[:, :, :, 1])
    asking_vectors_group = query_unit.astype(jnp.bfloat16)
    lookup_vectors_group = key_unit.astype(jnp.bfloat16)
    value_b = projected[:, :, :, 2].astype(jnp.bfloat16)
    similarity_table = normalizing_sharpness * jnp.einsum(
        "cfhd,cghd->chfg",
        asking_vectors_group,
        lookup_vectors_group,
        preferred_element_type=jnp.float32,
    )
    expo = jnp.exp(similarity_table)
    focus_probabilities = expo / jnp.sum(expo, axis=-1, keepdims=True)
    attention_b = focus_probabilities.astype(jnp.bfloat16)
    column_mass = jnp.sum(attention_b, axis=2, dtype=jnp.float32)
    value_f = value_b.astype(jnp.float32)
    pooled = jnp.einsum("chg,cghd->chd", column_mass, value_f, precision=highest)
    pooled_b = pooled.astype(jnp.bfloat16).reshape(clips_dev, D_REW)
    motion_emb = jnp.dot(
        pooled_b, proj_rows.astype(jnp.bfloat16), preferred_element_type=jnp.float32
    )
    prompts = lax.dynamic_slice_in_dim(prompt_index, me * clips_dev, clips_dev)
    weights = lax.dynamic_slice_in_dim(reward_weight, me * clips_dev, clips_dev)
    choose = (prompts[:, None] == jnp.arange(PROMPTS)[None, :]).astype(jnp.float32)
    target = jnp.dot(choose, text_unit, precision=highest)
    emb_len = jnp.sqrt(jnp.sum(motion_emb * motion_emb, axis=-1) + epsilon)
    rewards = jnp.sum(motion_emb * target, axis=-1) / emb_len
    d_memb = (
        (-weights)[:, None]
        * (target - rewards[:, None] * motion_emb / emb_len[:, None])
        / emb_len[:, None]
    )
    d_pooled = jnp.dot(d_memb, proj_rows.T, precision=highest).reshape(
        clips_dev, HEADS, head_size
    )
    reduction_dimension = jnp.einsum("chd,cghd->chg", d_pooled, value_f, precision=highest)
    d_value = jnp.transpose(column_mass, (0, 2, 1))[..., None] * d_pooled[:, None]
    pairwise_dot_similarity = jnp.sum(
        focus_probabilities * reduction_dimension[:, :, None, :], axis=-1, keepdims=True
    )
    similarity_derivative = (
        normalizing_sharpness
        * focus_probabilities
        * (reduction_dimension[:, :, None, :] - pairwise_dot_similarity)
    ).astype(jnp.bfloat16)
    d_qu = jnp.einsum(
        "chfg,cghd->cfhd",
        similarity_derivative,
        lookup_vectors_group,
        preferred_element_type=jnp.float32,
    )
    d_ku = jnp.einsum(
        "chfg,cfhd->cghd",
        similarity_derivative,
        asking_vectors_group,
        preferred_element_type=jnp.float32,
    )
    d_query = (d_qu - query_unit * jnp.sum(query_unit * d_qu, axis=-1, keepdims=True)) / query_len
    d_key = (d_ku - key_unit * jnp.sum(key_unit * d_ku, axis=-1, keepdims=True)) / key_len
    d_proj = jnp.stack([d_query, d_key, d_value], axis=3).astype(jnp.bfloat16)
    d_emb = jnp.einsum("cfhjk,hjdk->cfd", d_proj, w_all, preferred_element_type=jnp.float32)
    d_motion = motion_grad(d_emb, normed_e, scale_rms, x_clean, theta, embed_rows, root_rows)
    d_eps_b = (-level * d_motion).astype(jnp.bfloat16)
    d_mod = jnp.einsum("cfe,de->cfd", d_eps_b, w_out, preferred_element_type=jnp.float32)
    d_norm = d_mod * gain
    grad_hidden = (
        inv_std
        * (
            d_norm
            - jnp.mean(d_norm, axis=-1, keepdims=True)
            - normed_h * jnp.mean(d_norm * normed_h, axis=-1, keepdims=True)
        )
    ).astype(jnp.bfloat16)
    grad_term = jnp.einsum("cfd,cfe->de", modulated, d_eps_b, preferred_element_type=jnp.float32)

    rows_dev = w_out.shape[0] // ways
    cols = grad_term.shape[1]
    n_dp = lax.axis_size("dp")
    total_clips = clips_dev * ways * n_dp * lax.axis_size("sec")
    extra = -(-total_clips // cols)
    extra = -(-extra // 8) * 8
    first_clip = (
        (lax.axis_index("sec") * n_dp + lax.axis_index("dp")) * ways + me
    ) * clips_dev
    columns = jnp.arange(extra * cols)
    slots = columns[None, :] == (first_clip + jnp.arange(clips_dev))[:, None]
    reward_rows = jnp.sum(jnp.where(slots, rewards[:, None], 0.0), axis=0).reshape(extra, cols)
    stacked = jnp.concatenate(
        [
            grad_term.reshape(ways, rows_dev, cols),
            jnp.broadcast_to(reward_rows[None], (ways, extra, cols)),
        ],
        axis=1,
    )
    block = halving_sum(stacked, "seq")
    block = doubling_sum(doubling_sum(block, "sec"), "dp")
    grad_w_out = block[:rows_dev]
    group_first = (lax.axis_index("sec") * n_dp + lax.axis_index("dp")) * ways * clips_dev
    all_rewards = block[rows_dev:].reshape(extra * cols)
    rewards_out = lax.dynamic_slice_in_dim(all_rewards, group_first, ways * clips_dev)
    return (rewards_out, grad_w_out, grad_hidden)


def solution(mesh):
    placed = (
        P(("sec", "dp", "seq"), None, None),
        P(("sec", "dp", "seq"), None),
        P(("sec", "dp", "seq"), None),
        P(("sec", "dp", "seq"), None, None),
        P(("sec", "dp", "seq")),
        P(),
        P(),
        P(),
        P(None, None, "seq"),
        P("seq", None),
        P("seq", None),
        P(),
        P(("sec", "dp")),
        P(("sec", "dp")),
    )
    return jax.shard_map(
        local,
        mesh=mesh,
        in_specs=placed,
        out_specs=(P(("sec", "dp")), P("seq", None), P(("sec", "dp", "seq"), None, None)),
        check_vma=False,
    )
```

```python
import jax
import jax.numpy as jnp
from jax import lax
from jax.sharding import PartitionSpec as P

D_REW = 2048
HEADS = 16
PROMPTS = 32


normalizing_sharpness = 10.0
epsilon = 1e-06
highest = lax.Precision.HIGHEST


def rotate(angle, first, second):
    cosine = jnp.cos(angle)
    sine_term = jnp.sin(angle)
    return (cosine * first + sine_term * second, cosine * second - sine_term * first)


def suffix(values):
    return jnp.sum(values, axis=1, keepdims=True) - jnp.cumsum(values, axis=1)


def local_path(motion):
    spin = motion[..., 0]
    theta = jnp.cumsum(spin, axis=1) - spin
    step_east, step_north = rotate(theta, motion[..., 1], motion[..., 2])
    path_east = jnp.cumsum(step_east, axis=1) - step_east
    path_north = jnp.cumsum(step_north, axis=1) - step_north
    return (theta, path_east, path_north)


def embed(motion, root_east, root_north, w_embed, root_rows):
    emb = jnp.einsum(
        "cfe,ed->cfd", motion.astype(jnp.bfloat16), w_embed, preferred_element_type=jnp.float32
    )
    emb = emb + root_east[..., None] * root_rows[0] + root_north[..., None] * root_rows[1]
    scale_rms = jnp.sqrt(jnp.mean(emb * emb, axis=-1, keepdims=True) + epsilon)
    return (emb / scale_rms, scale_rms)


def unit_rows(vectors):
    length = jnp.sqrt(jnp.sum(vectors * vectors, axis=-1, keepdims=True) + epsilon)
    return (vectors / length, length)


def norm_grad(grad, normed, scale_rms):
    return (grad - normed * jnp.mean(grad * normed, axis=-1, keepdims=True)) / scale_rms


def motion_grad(d_emb, normed_e, scale_rms, motion, theta, embed_rows, root_rows):
    d_unemb = norm_grad(d_emb, normed_e, scale_rms)
    d_embedded = jnp.einsum("cfd,ed->cfe", d_unemb, embed_rows, precision=highest)
    grad_east = suffix(jnp.sum(d_unemb * root_rows[0], axis=-1))
    grad_north = suffix(jnp.sum(d_unemb * root_rows[1], axis=-1))
    vel_east = motion[..., 1]
    vel_north = motion[..., 2]
    d_east, d_north = rotate(-theta, grad_east, grad_north)
    cosine = jnp.cos(theta)
    sine_term = jnp.sin(theta)
    d_theta = grad_east * (cosine * vel_north - sine_term * vel_east) - grad_north * (
        cosine * vel_east + sine_term * vel_north
    )
    d_spin = suffix(d_theta)
    return d_embedded.at[..., 0].add(d_spin).at[..., 1].add(d_east).at[..., 2].add(d_north)


def xor_pairs(size, bit):
    return [(i, i ^ bit) for i in range(size)]


def halving_sum(chunks, axis, wire_types):
    size = lax.axis_size(axis)
    me = lax.axis_index(axis)
    bits = size.bit_length() - 1
    assert 1 << bits == size
    buf = chunks.reshape((2,) * bits + chunks.shape[1:])
    for k in range(bits):
        mine = (me >> k) & 1
        keep = lax.dynamic_index_in_dim(buf, mine, axis=bits - 1 - k, keepdims=False)
        send = lax.dynamic_index_in_dim(buf, 1 - mine, axis=bits - 1 - k, keepdims=False)
        got = lax.ppermute(send.astype(wire_types[k]), axis, xor_pairs(size, 1 << k))
        buf = keep + got.astype(keep.dtype)
    return buf


def doubling_sum(value, axis):
    size = lax.axis_size(axis)
    bits = size.bit_length() - 1
    assert 1 << bits == size
    for k in range(bits):
        value = value + lax.ppermute(value, axis, xor_pairs(size, 1 << k))
    return value


def local(
    hidden,
    cond_shift,
    cond_scale,
    noisy,
    noise_level,
    w_out,
    w_embed,
    w_root,
    w_qkv,
    w_proj,
    text_table,
    text_ids,
    prompt_index,
    reward_weight,
):
    clips_dev = hidden.shape[0]
    ways = lax.axis_size("seq")
    me = lax.axis_index("seq")
    head_size = D_REW // HEADS
    root_rows = w_root.astype(jnp.float32)
    embed_rows = w_embed.astype(jnp.float32)

    vocab_rows = text_table.shape[0]
    local_ids = text_ids - me * vocab_rows
    inside = (local_ids >= 0) & (local_ids < vocab_rows)
    picked = jnp.take(text_table, jnp.clip(local_ids, 0, vocab_rows - 1), axis=0).astype(
        jnp.float32
    )
    text_part = jnp.sum(jnp.where(inside[..., None], picked, 0.0), axis=1)
    text_raw = doubling_sum(text_part, "seq")
    w_all = lax.all_gather(w_qkv, "seq", axis=0)

    hidden_f = hidden.astype(jnp.float32)
    centred = hidden_f - jnp.mean(hidden_f, axis=-1, keepdims=True)
    inv_std = lax.rsqrt(jnp.mean(centred * centred, axis=-1, keepdims=True) + epsilon)
    normed_h = centred * inv_std
    gain = 1.0 + cond_scale.astype(jnp.float32)[:, None, :]
    modulated = (normed_h * gain + cond_shift.astype(jnp.float32)[:, None, :]).astype(jnp.bfloat16)
    eps_pred = jnp.einsum("cfd,de->cfe", modulated, w_out, preferred_element_type=jnp.float32)
    level = noise_level[:, None, None]
    x_clean = noisy.astype(jnp.float32) - level * eps_pred
    theta, path_east, path_north = local_path(x_clean)
    normed_e, scale_rms = embed(x_clean, path_east, path_north, w_embed, root_rows)
    w_all, proj_send, emb_b, text_raw = lax.optimization_barrier(
        (w_all, w_proj, normed_e.astype(jnp.bfloat16), text_raw)
    )
    text_unit, text_len = unit_rows(text_raw)
    proj_b = lax.all_gather(proj_send, "seq", axis=0, tiled=True)
    proj_rows = proj_b.astype(jnp.float32)
    projected = jnp.einsum(
        "cfd,hjdk->cfhjk",
        emb_b,
        w_all,
        preferred_element_type=jnp.float32,
    )
    query_unit, query_len = unit_rows(projected[:, :, :, 0])
    key_unit, key_len = unit_rows(projected[:, :, :, 1])
    asking_vectors_group = query_unit.astype(jnp.bfloat16)
    lookup_vectors_group = key_unit.astype(jnp.bfloat16)
    value_b = projected[:, :, :, 2].astype(jnp.bfloat16)
    similarity_table = normalizing_sharpness * jnp.einsum(
        "cfhd,cghd->chfg",
        asking_vectors_group,
        lookup_vectors_group,
        preferred_element_type=jnp.float32,
    )
    expo = jnp.exp(similarity_table)
    focus_probabilities = expo / jnp.sum(expo, axis=-1, keepdims=True)
    attention_b = focus_probabilities.astype(jnp.bfloat16)
    column_mass = jnp.sum(attention_b, axis=2, dtype=jnp.float32)
    value_f = value_b.astype(jnp.float32)
    pooled = jnp.einsum("chg,cghd->chd", column_mass, value_f, precision=highest)
    pooled_b = pooled.astype(jnp.bfloat16).reshape(clips_dev, D_REW)
    motion_emb = jnp.dot(pooled_b, proj_b, preferred_element_type=jnp.float32)
    prompts = lax.dynamic_slice_in_dim(prompt_index, me * clips_dev, clips_dev)
    weights = lax.dynamic_slice_in_dim(reward_weight, me * clips_dev, clips_dev)
    choose = (prompts[:, None] == jnp.arange(PROMPTS)[None, :]).astype(jnp.float32)
    target = jnp.dot(choose, text_unit, precision=highest)
    emb_len = jnp.sqrt(jnp.sum(motion_emb * motion_emb, axis=-1) + epsilon)
    rewards = jnp.sum(motion_emb * target, axis=-1) / emb_len
    d_memb = (
        (-weights)[:, None]
        * (target - rewards[:, None] * motion_emb / emb_len[:, None])
        / emb_len[:, None]
    )
    d_pooled = jnp.dot(d_memb, proj_rows.T, precision=highest).reshape(
        clips_dev, HEADS, head_size
    )
    reduction_dimension = jnp.einsum("chd,cghd->chg", d_pooled, value_f, precision=highest)
    d_value = jnp.transpose(column_mass, (0, 2, 1))[..., None] * d_pooled[:, None]
    pairwise_dot_similarity = jnp.sum(
        focus_probabilities * reduction_dimension[:, :, None, :], axis=-1, keepdims=True
    )
    similarity_derivative = (
        normalizing_sharpness
        * focus_probabilities
        * (reduction_dimension[:, :, None, :] - pairwise_dot_similarity)
    ).astype(jnp.bfloat16)
    d_qu = jnp.einsum(
        "chfg,cghd->cfhd",
        similarity_derivative,
        lookup_vectors_group,
        preferred_element_type=jnp.float32,
    )
    d_ku = jnp.einsum(
        "chfg,cfhd->cghd",
        similarity_derivative,
        asking_vectors_group,
        preferred_element_type=jnp.float32,
    )
    d_query = (d_qu - query_unit * jnp.sum(query_unit * d_qu, axis=-1, keepdims=True)) / query_len
    d_key = (d_ku - key_unit * jnp.sum(key_unit * d_ku, axis=-1, keepdims=True)) / key_len
    d_proj = jnp.stack([d_query, d_key, d_value], axis=3).astype(jnp.bfloat16)
    d_emb = jnp.einsum("cfhjk,hjdk->cfd", d_proj, w_all, preferred_element_type=jnp.float32)
    d_motion = motion_grad(d_emb, normed_e, scale_rms, x_clean, theta, embed_rows, root_rows)
    d_eps_b = (-level * d_motion).astype(jnp.bfloat16)
    d_mod = jnp.einsum("cfe,de->cfd", d_eps_b, w_out, preferred_element_type=jnp.float32)
    d_norm = d_mod * gain
    grad_hidden = (
        inv_std
        * (
            d_norm
            - jnp.mean(d_norm, axis=-1, keepdims=True)
            - normed_h * jnp.mean(d_norm * normed_h, axis=-1, keepdims=True)
        )
    ).astype(jnp.bfloat16)
    grad_term = jnp.einsum("cfd,cfe->de", modulated, d_eps_b, preferred_element_type=jnp.float32)

    rows_dev = w_out.shape[0] // ways
    cols = grad_term.shape[1]
    n_dp = lax.axis_size("dp")
    total_clips = clips_dev * ways * n_dp * lax.axis_size("sec")
    extra = -(-total_clips // cols)
    extra = -(-extra // 8) * 8
    first_clip = (
        (lax.axis_index("sec") * n_dp + lax.axis_index("dp")) * ways + me
    ) * clips_dev
    columns = jnp.arange(extra * cols)
    slots = columns[None, :] == (first_clip + jnp.arange(clips_dev))[:, None]
    reward_rows = jnp.sum(jnp.where(slots, rewards[:, None], 0.0), axis=0).reshape(extra, cols)
    stacked = jnp.concatenate(
        [
            grad_term.reshape(ways, rows_dev, cols),
            jnp.broadcast_to(reward_rows[None], (ways, extra, cols)),
        ],
        axis=1,
    )
    seq_bits = ways.bit_length() - 1
    block = halving_sum(stacked, "seq", [jnp.float32] + [jnp.bfloat16] * (seq_bits - 1))
    block = doubling_sum(doubling_sum(block, "sec"), "dp")
    grad_w_out = block[:rows_dev]
    group_first = (lax.axis_index("sec") * n_dp + lax.axis_index("dp")) * ways * clips_dev
    all_rewards = block[rows_dev:].reshape(extra * cols)
    rewards_out = lax.dynamic_slice_in_dim(all_rewards, group_first, ways * clips_dev)
    return (rewards_out, grad_w_out, grad_hidden)


def solution(mesh):
    placed = (
        P(("sec", "dp", "seq"), None, None),
        P(("sec", "dp", "seq"), None),
        P(("sec", "dp", "seq"), None),
        P(("sec", "dp", "seq"), None, None),
        P(("sec", "dp", "seq")),
        P(),
        P(),
        P(),
        P(None, None, "seq"),
        P("seq", None),
        P("seq", None),
        P(),
        P(("sec", "dp")),
        P(("sec", "dp")),
    )
    return jax.shard_map(
        local,
        mesh=mesh,
        in_specs=placed,
        out_specs=(P(("sec", "dp")), P("seq", None), P(("sec", "dp", "seq"), None, None)),
        check_vma=False,
    )
```

```python
import jax
import jax.numpy as jnp
from jax import lax
from jax.sharding import PartitionSpec as P

D_REW = 2048
HEADS = 16
PROMPTS = 32


normalizing_sharpness = 10.0
epsilon = 1e-06
highest = lax.Precision.HIGHEST


def rotate(angle, first, second):
    cosine = jnp.cos(angle)
    sine_term = jnp.sin(angle)
    return (cosine * first + sine_term * second, cosine * second - sine_term * first)


def suffix(values):
    return jnp.sum(values, axis=1, keepdims=True) - jnp.cumsum(values, axis=1)


def local_path(motion):
    spin = motion[..., 0]
    theta = jnp.cumsum(spin, axis=1) - spin
    step_east, step_north = rotate(theta, motion[..., 1], motion[..., 2])
    path_east = jnp.cumsum(step_east, axis=1) - step_east
    path_north = jnp.cumsum(step_north, axis=1) - step_north
    return (theta, path_east, path_north)


def embed(motion, root_east, root_north, w_embed, root_rows):
    emb = jnp.einsum(
        "cfe,ed->cfd", motion.astype(jnp.bfloat16), w_embed, preferred_element_type=jnp.float32
    )
    emb = emb + root_east[..., None] * root_rows[0] + root_north[..., None] * root_rows[1]
    scale_rms = jnp.sqrt(jnp.mean(emb * emb, axis=-1, keepdims=True) + epsilon)
    return (emb / scale_rms, scale_rms)


def unit_rows(vectors):
    length = jnp.sqrt(jnp.sum(vectors * vectors, axis=-1, keepdims=True) + epsilon)
    return (vectors / length, length)


def norm_grad(grad, normed, scale_rms):
    return (grad - normed * jnp.mean(grad * normed, axis=-1, keepdims=True)) / scale_rms


def motion_grad(d_emb, normed_e, scale_rms, motion, theta, embed_rows, root_rows):
    d_unemb = norm_grad(d_emb, normed_e, scale_rms)
    d_embedded = jnp.einsum("cfd,ed->cfe", d_unemb, embed_rows, precision=highest)
    grad_east = suffix(jnp.sum(d_unemb * root_rows[0], axis=-1))
    grad_north = suffix(jnp.sum(d_unemb * root_rows[1], axis=-1))
    vel_east = motion[..., 1]
    vel_north = motion[..., 2]
    d_east, d_north = rotate(-theta, grad_east, grad_north)
    cosine = jnp.cos(theta)
    sine_term = jnp.sin(theta)
    d_theta = grad_east * (cosine * vel_north - sine_term * vel_east) - grad_north * (
        cosine * vel_east + sine_term * vel_north
    )
    d_spin = suffix(d_theta)
    return d_embedded.at[..., 0].add(d_spin).at[..., 1].add(d_east).at[..., 2].add(d_north)


def xor_pairs(size, bit):
    return [(i, i ^ bit) for i in range(size)]


def halving_sum(chunks, axis, wire_types):
    size = lax.axis_size(axis)
    me = lax.axis_index(axis)
    bits = size.bit_length() - 1
    assert 1 << bits == size
    buf = chunks.reshape((2,) * bits + chunks.shape[1:])
    for k in range(bits):
        mine = (me >> k) & 1
        keep = lax.dynamic_index_in_dim(buf, mine, axis=bits - 1 - k, keepdims=False)
        send = lax.dynamic_index_in_dim(buf, 1 - mine, axis=bits - 1 - k, keepdims=False)
        got = lax.ppermute(send.astype(wire_types[k]), axis, xor_pairs(size, 1 << k))
        buf = keep + got.astype(keep.dtype)
    return buf


def doubling_gather(value, axis):
    size = lax.axis_size(axis)
    me = lax.axis_index(axis)
    bits = size.bit_length() - 1
    assert 1 << bits == size
    held = value[None]
    for k in reversed(range(bits)):
        held = jnp.concatenate([held, lax.ppermute(held, axis, xor_pairs(size, 1 << k))], axis=0)
    wanted = jnp.arange(size) ^ me
    position = sum(((wanted >> k) & 1) << (bits - 1 - k) for k in range(bits))
    return jnp.take(held, position, axis=0)


def doubling_sum(value, axis):
    size = lax.axis_size(axis)
    bits = size.bit_length() - 1
    assert 1 << bits == size
    for k in range(bits):
        value = value + lax.ppermute(value, axis, xor_pairs(size, 1 << k))
    return value


def local(
    hidden,
    cond_shift,
    cond_scale,
    noisy,
    noise_level,
    w_out,
    w_embed,
    w_root,
    w_qkv,
    w_proj,
    text_table,
    text_ids,
    prompt_index,
    reward_weight,
):
    clips_dev = hidden.shape[0]
    ways = lax.axis_size("seq")
    me = lax.axis_index("seq")
    head_size = D_REW // HEADS
    root_rows = w_root.astype(jnp.float32)
    embed_rows = w_embed.astype(jnp.float32)

    vocab_rows = text_table.shape[0]
    local_ids = text_ids - me * vocab_rows
    inside = (local_ids >= 0) & (local_ids < vocab_rows)
    picked = jnp.take(text_table, jnp.clip(local_ids, 0, vocab_rows - 1), axis=0).astype(
        jnp.float32
    )
    text_part = jnp.sum(jnp.where(inside[..., None], picked, 0.0), axis=1)
    text_raw = doubling_sum(text_part, "seq")
    w_all = lax.all_gather(w_qkv, "seq", axis=0)

    hidden_f = hidden.astype(jnp.float32)
    centred = hidden_f - jnp.mean(hidden_f, axis=-1, keepdims=True)
    inv_std = lax.rsqrt(jnp.mean(centred * centred, axis=-1, keepdims=True) + epsilon)
    normed_h = centred * inv_std
    gain = 1.0 + cond_scale.astype(jnp.float32)[:, None, :]
    modulated = (normed_h * gain + cond_shift.astype(jnp.float32)[:, None, :]).astype(jnp.bfloat16)
    eps_pred = jnp.einsum("cfd,de->cfe", modulated, w_out, preferred_element_type=jnp.float32)
    level = noise_level[:, None, None]
    x_clean = noisy.astype(jnp.float32) - level * eps_pred
    theta, path_east, path_north = local_path(x_clean)
    normed_e, scale_rms = embed(x_clean, path_east, path_north, w_embed, root_rows)
    proj_b = doubling_gather(w_proj, "seq").reshape(ways * w_proj.shape[0], w_proj.shape[1])
    w_all, proj_b, emb_b, text_raw = lax.optimization_barrier(
        (w_all, proj_b, normed_e.astype(jnp.bfloat16), text_raw)
    )
    text_unit, text_len = unit_rows(text_raw)
    proj_rows = proj_b.astype(jnp.float32)
    projected = jnp.einsum(
        "cfd,hjdk->cfhjk",
        emb_b,
        w_all,
        preferred_element_type=jnp.float32,
    )
    query_unit, query_len = unit_rows(projected[:, :, :, 0])
    key_unit, key_len = unit_rows(projected[:, :, :, 1])
    asking_vectors_group = query_unit.astype(jnp.bfloat16)
    lookup_vectors_group = key_unit.astype(jnp.bfloat16)
    value_b = projected[:, :, :, 2].astype(jnp.bfloat16)
    similarity_table = normalizing_sharpness * jnp.einsum(
        "cfhd,cghd->chfg",
        asking_vectors_group,
        lookup_vectors_group,
        preferred_element_type=jnp.float32,
    )
    expo = jnp.exp(similarity_table)
    focus_probabilities = expo / jnp.sum(expo, axis=-1, keepdims=True)
    attention_b = focus_probabilities.astype(jnp.bfloat16)
    column_mass = jnp.sum(attention_b, axis=2, dtype=jnp.float32)
    value_f = value_b.astype(jnp.float32)
    pooled = jnp.einsum("chg,cghd->chd", column_mass, value_f, precision=highest)
    pooled_b = pooled.astype(jnp.bfloat16).reshape(clips_dev, D_REW)
    motion_emb = jnp.dot(pooled_b, proj_b, preferred_element_type=jnp.float32)
    prompts = lax.dynamic_slice_in_dim(prompt_index, me * clips_dev, clips_dev)
    weights = lax.dynamic_slice_in_dim(reward_weight, me * clips_dev, clips_dev)
    choose = (prompts[:, None] == jnp.arange(PROMPTS)[None, :]).astype(jnp.float32)
    target = jnp.dot(choose, text_unit, precision=highest)
    emb_len = jnp.sqrt(jnp.sum(motion_emb * motion_emb, axis=-1) + epsilon)
    rewards = jnp.sum(motion_emb * target, axis=-1) / emb_len
    d_memb = (
        (-weights)[:, None]
        * (target - rewards[:, None] * motion_emb / emb_len[:, None])
        / emb_len[:, None]
    )
    d_pooled = jnp.dot(d_memb, proj_rows.T, precision=highest).reshape(
        clips_dev, HEADS, head_size
    )
    reduction_dimension = jnp.einsum("chd,cghd->chg", d_pooled, value_f, precision=highest)
    d_value = jnp.transpose(column_mass, (0, 2, 1))[..., None] * d_pooled[:, None]
    pairwise_dot_similarity = jnp.sum(
        focus_probabilities * reduction_dimension[:, :, None, :], axis=-1, keepdims=True
    )
    similarity_derivative = (
        normalizing_sharpness
        * focus_probabilities
        * (reduction_dimension[:, :, None, :] - pairwise_dot_similarity)
    ).astype(jnp.bfloat16)
    d_qu = jnp.einsum(
        "chfg,cghd->cfhd",
        similarity_derivative,
        lookup_vectors_group,
        preferred_element_type=jnp.float32,
    )
    d_ku = jnp.einsum(
        "chfg,cfhd->cghd",
        similarity_derivative,
        asking_vectors_group,
        preferred_element_type=jnp.float32,
    )
    d_query = (d_qu - query_unit * jnp.sum(query_unit * d_qu, axis=-1, keepdims=True)) / query_len
    d_key = (d_ku - key_unit * jnp.sum(key_unit * d_ku, axis=-1, keepdims=True)) / key_len
    d_proj = jnp.stack([d_query, d_key, d_value], axis=3).astype(jnp.bfloat16)
    d_emb = jnp.einsum("cfhjk,hjdk->cfd", d_proj, w_all, preferred_element_type=jnp.float32)
    d_motion = motion_grad(d_emb, normed_e, scale_rms, x_clean, theta, embed_rows, root_rows)
    d_eps_b = (-level * d_motion).astype(jnp.bfloat16)
    d_mod = jnp.einsum("cfe,de->cfd", d_eps_b, w_out, preferred_element_type=jnp.float32)
    d_norm = d_mod * gain
    grad_hidden = (
        inv_std
        * (
            d_norm
            - jnp.mean(d_norm, axis=-1, keepdims=True)
            - normed_h * jnp.mean(d_norm * normed_h, axis=-1, keepdims=True)
        )
    ).astype(jnp.bfloat16)
    grad_term = jnp.einsum("cfd,cfe->de", modulated, d_eps_b, preferred_element_type=jnp.float32)

    rows_dev = w_out.shape[0] // ways
    cols = grad_term.shape[1]
    n_dp = lax.axis_size("dp")
    total_clips = clips_dev * ways * n_dp * lax.axis_size("sec")
    extra = -(-total_clips // cols)
    extra = -(-extra // 8) * 8
    first_clip = (
        (lax.axis_index("sec") * n_dp + lax.axis_index("dp")) * ways + me
    ) * clips_dev
    columns = jnp.arange(extra * cols)
    slots = columns[None, :] == (first_clip + jnp.arange(clips_dev))[:, None]
    reward_rows = jnp.sum(jnp.where(slots, rewards[:, None], 0.0), axis=0).reshape(extra, cols)
    stacked = jnp.concatenate(
        [
            grad_term.reshape(ways, rows_dev, cols),
            jnp.broadcast_to(reward_rows[None], (ways, extra, cols)),
        ],
        axis=1,
    )
    seq_bits = ways.bit_length() - 1
    block = halving_sum(stacked, "seq", [jnp.float32] + [jnp.bfloat16] * (seq_bits - 1))
    block = doubling_sum(doubling_sum(block, "sec"), "dp")
    grad_w_out = block[:rows_dev]
    group_first = (lax.axis_index("sec") * n_dp + lax.axis_index("dp")) * ways * clips_dev
    all_rewards = block[rows_dev:].reshape(extra * cols)
    rewards_out = lax.dynamic_slice_in_dim(all_rewards, group_first, ways * clips_dev)
    return (rewards_out, grad_w_out, grad_hidden)


def solution(mesh):
    placed = (
        P(("sec", "dp", "seq"), None, None),
        P(("sec", "dp", "seq"), None),
        P(("sec", "dp", "seq"), None),
        P(("sec", "dp", "seq"), None, None),
        P(("sec", "dp", "seq")),
        P(),
        P(),
        P(),
        P(None, None, "seq"),
        P("seq", None),
        P("seq", None),
        P(),
        P(("sec", "dp")),
        P(("sec", "dp")),
    )
    return jax.shard_map(
        local,
        mesh=mesh,
        in_specs=placed,
        out_specs=(P(("sec", "dp")), P("seq", None), P(("sec", "dp", "seq"), None, None)),
        check_vma=False,
    )
```

```python
import jax
import jax.numpy as jnp
from jax import lax
from jax.sharding import PartitionSpec as P

D_REW = 2048
HEADS = 16
PROMPTS = 32


normalizing_sharpness = 10.0
epsilon = 1e-06
highest = lax.Precision.HIGHEST


def rotate(angle, first, second):
    cosine = jnp.cos(angle)
    sine_term = jnp.sin(angle)
    return (cosine * first + sine_term * second, cosine * second - sine_term * first)


def suffix(values):
    return jnp.sum(values, axis=1, keepdims=True) - jnp.cumsum(values, axis=1)


def local_path(motion):
    spin = motion[..., 0]
    theta = jnp.cumsum(spin, axis=1) - spin
    step_east, step_north = rotate(theta, motion[..., 1], motion[..., 2])
    path_east = jnp.cumsum(step_east, axis=1) - step_east
    path_north = jnp.cumsum(step_north, axis=1) - step_north
    return (theta, path_east, path_north)


def embed(motion, root_east, root_north, w_embed, root_rows):
    emb = jnp.einsum(
        "cfe,ed->cfd", motion.astype(jnp.bfloat16), w_embed, preferred_element_type=jnp.float32
    )
    emb = emb + root_east[..., None] * root_rows[0] + root_north[..., None] * root_rows[1]
    scale_rms = jnp.sqrt(jnp.mean(emb * emb, axis=-1, keepdims=True) + epsilon)
    return (emb / scale_rms, scale_rms)


def unit_rows(vectors):
    length = jnp.sqrt(jnp.sum(vectors * vectors, axis=-1, keepdims=True) + epsilon)
    return (vectors / length, length)


def norm_grad(grad, normed, scale_rms):
    return (grad - normed * jnp.mean(grad * normed, axis=-1, keepdims=True)) / scale_rms


def motion_grad(d_emb, normed_e, scale_rms, motion, theta, embed_rows, root_rows):
    d_unemb = norm_grad(d_emb, normed_e, scale_rms)
    d_embedded = jnp.einsum("cfd,ed->cfe", d_unemb, embed_rows, precision=highest)
    grad_east = suffix(jnp.sum(d_unemb * root_rows[0], axis=-1))
    grad_north = suffix(jnp.sum(d_unemb * root_rows[1], axis=-1))
    vel_east = motion[..., 1]
    vel_north = motion[..., 2]
    d_east, d_north = rotate(-theta, grad_east, grad_north)
    cosine = jnp.cos(theta)
    sine_term = jnp.sin(theta)
    d_theta = grad_east * (cosine * vel_north - sine_term * vel_east) - grad_north * (
        cosine * vel_east + sine_term * vel_north
    )
    d_spin = suffix(d_theta)
    return d_embedded.at[..., 0].add(d_spin).at[..., 1].add(d_east).at[..., 2].add(d_north)


def xor_pairs(size, bit):
    return [(i, i ^ bit) for i in range(size)]


def halving_sum(chunks, axis, wire_types):
    size = lax.axis_size(axis)
    me = lax.axis_index(axis)
    bits = size.bit_length() - 1
    assert 1 << bits == size
    buf = chunks.reshape((2,) * bits + chunks.shape[1:])
    for k in range(bits):
        mine = (me >> k) & 1
        keep = lax.dynamic_index_in_dim(buf, mine, axis=bits - 1 - k, keepdims=False)
        send = lax.dynamic_index_in_dim(buf, 1 - mine, axis=bits - 1 - k, keepdims=False)
        got = lax.ppermute(send.astype(wire_types[k]), axis, xor_pairs(size, 1 << k))
        buf = keep + got.astype(keep.dtype)
    return buf


def quad_sum(value, axes, low_bit, high_bit):
    size = 1
    for axis in axes:
        size *= lax.axis_size(axis)
    me = 0
    for axis in axes:
        me = me * lax.axis_size(axis) + lax.axis_index(axis)
    offsets = [0, 1 << low_bit, 1 << high_bit, (1 << low_bit) | (1 << high_bit)]
    vals = [value] + [lax.ppermute(value, axes, xor_pairs(size, d)) for d in offsets[1:]]
    position = ((me >> low_bit) & 1) + 2 * ((me >> high_bit) & 1)
    members = jnp.take(jnp.stack(vals), jnp.arange(4) ^ position, axis=0)
    return (members[0] + members[1]) + (members[2] + members[3])


def doubling_sum(value, axis):
    size = lax.axis_size(axis)
    bits = size.bit_length() - 1
    assert 1 << bits == size
    for k in range(bits):
        value = value + lax.ppermute(value, axis, xor_pairs(size, 1 << k))
    return value


def local(
    hidden,
    cond_shift,
    cond_scale,
    noisy,
    noise_level,
    w_out,
    w_embed,
    w_root,
    w_qkv,
    w_proj,
    text_table,
    text_ids,
    prompt_index,
    reward_weight,
):
    clips_dev = hidden.shape[0]
    ways = lax.axis_size("seq")
    me = lax.axis_index("seq")
    head_size = D_REW // HEADS
    root_rows = w_root.astype(jnp.float32)
    embed_rows = w_embed.astype(jnp.float32)

    vocab_rows = text_table.shape[0]
    local_ids = text_ids - me * vocab_rows
    inside = (local_ids >= 0) & (local_ids < vocab_rows)
    picked = jnp.take(text_table, jnp.clip(local_ids, 0, vocab_rows - 1), axis=0).astype(
        jnp.float32
    )
    text_part = jnp.sum(jnp.where(inside[..., None], picked, 0.0), axis=1)
    text_raw = doubling_sum(text_part, "seq")
    w_all = lax.all_gather(w_qkv, "seq", axis=0)

    hidden_f = hidden.astype(jnp.float32)
    centred = hidden_f - jnp.mean(hidden_f, axis=-1, keepdims=True)
    inv_std = lax.rsqrt(jnp.mean(centred * centred, axis=-1, keepdims=True) + epsilon)
    normed_h = centred * inv_std
    gain = 1.0 + cond_scale.astype(jnp.float32)[:, None, :]
    modulated = (normed_h * gain + cond_shift.astype(jnp.float32)[:, None, :]).astype(jnp.bfloat16)
    eps_pred = jnp.einsum("cfd,de->cfe", modulated, w_out, preferred_element_type=jnp.float32)
    level = noise_level[:, None, None]
    x_clean = noisy.astype(jnp.float32) - level * eps_pred
    theta, path_east, path_north = local_path(x_clean)
    normed_e, scale_rms = embed(x_clean, path_east, path_north, w_embed, root_rows)
    w_all, proj_send, emb_b, text_raw = lax.optimization_barrier(
        (w_all, w_proj, normed_e.astype(jnp.bfloat16), text_raw)
    )
    text_unit, text_len = unit_rows(text_raw)
    proj_b = lax.all_gather(proj_send, "seq", axis=0, tiled=True)
    proj_rows = proj_b.astype(jnp.float32)
    projected = jnp.einsum(
        "cfd,hjdk->cfhjk",
        emb_b,
        w_all,
        preferred_element_type=jnp.float32,
    )
    query_unit, query_len = unit_rows(projected[:, :, :, 0])
    key_unit, key_len = unit_rows(projected[:, :, :, 1])
    asking_vectors_group = query_unit.astype(jnp.bfloat16)
    lookup_vectors_group = key_unit.astype(jnp.bfloat16)
    value_b = projected[:, :, :, 2].astype(jnp.bfloat16)
    similarity_table = normalizing_sharpness * jnp.einsum(
        "cfhd,cghd->chfg",
        asking_vectors_group,
        lookup_vectors_group,
        preferred_element_type=jnp.float32,
    )
    expo = jnp.exp(similarity_table)
    focus_probabilities = expo / jnp.sum(expo, axis=-1, keepdims=True)
    attention_b = focus_probabilities.astype(jnp.bfloat16)
    column_mass = jnp.sum(attention_b, axis=2, dtype=jnp.float32)
    value_f = value_b.astype(jnp.float32)
    pooled = jnp.einsum("chg,cghd->chd", column_mass, value_f, precision=highest)
    pooled_b = pooled.astype(jnp.bfloat16).reshape(clips_dev, D_REW)
    motion_emb = jnp.dot(pooled_b, proj_b, preferred_element_type=jnp.float32)
    prompts = lax.dynamic_slice_in_dim(prompt_index, me * clips_dev, clips_dev)
    weights = lax.dynamic_slice_in_dim(reward_weight, me * clips_dev, clips_dev)
    choose = (prompts[:, None] == jnp.arange(PROMPTS)[None, :]).astype(jnp.float32)
    target = jnp.dot(choose, text_unit, precision=highest)
    emb_len = jnp.sqrt(jnp.sum(motion_emb * motion_emb, axis=-1) + epsilon)
    rewards = jnp.sum(motion_emb * target, axis=-1) / emb_len
    d_memb = (
        (-weights)[:, None]
        * (target - rewards[:, None] * motion_emb / emb_len[:, None])
        / emb_len[:, None]
    )
    d_pooled = jnp.dot(d_memb, proj_rows.T, precision=highest).reshape(
        clips_dev, HEADS, head_size
    )
    reduction_dimension = jnp.einsum("chd,cghd->chg", d_pooled, value_f, precision=highest)
    d_value = jnp.transpose(column_mass, (0, 2, 1))[..., None] * d_pooled[:, None]
    pairwise_dot_similarity = jnp.sum(
        focus_probabilities * reduction_dimension[:, :, None, :], axis=-1, keepdims=True
    )
    similarity_derivative = (
        normalizing_sharpness
        * focus_probabilities
        * (reduction_dimension[:, :, None, :] - pairwise_dot_similarity)
    ).astype(jnp.bfloat16)
    d_qu = jnp.einsum(
        "chfg,cghd->cfhd",
        similarity_derivative,
        lookup_vectors_group,
        preferred_element_type=jnp.float32,
    )
    d_ku = jnp.einsum(
        "chfg,cfhd->cghd",
        similarity_derivative,
        asking_vectors_group,
        preferred_element_type=jnp.float32,
    )
    d_query = (d_qu - query_unit * jnp.sum(query_unit * d_qu, axis=-1, keepdims=True)) / query_len
    d_key = (d_ku - key_unit * jnp.sum(key_unit * d_ku, axis=-1, keepdims=True)) / key_len
    d_proj = jnp.stack([d_query, d_key, d_value], axis=3).astype(jnp.bfloat16)
    d_emb = jnp.einsum("cfhjk,hjdk->cfd", d_proj, w_all, preferred_element_type=jnp.float32)
    d_motion = motion_grad(d_emb, normed_e, scale_rms, x_clean, theta, embed_rows, root_rows)
    d_eps_b = (-level * d_motion).astype(jnp.bfloat16)
    d_mod = jnp.einsum("cfe,de->cfd", d_eps_b, w_out, preferred_element_type=jnp.float32)
    d_norm = d_mod * gain
    grad_hidden = (
        inv_std
        * (
            d_norm
            - jnp.mean(d_norm, axis=-1, keepdims=True)
            - normed_h * jnp.mean(d_norm * normed_h, axis=-1, keepdims=True)
        )
    ).astype(jnp.bfloat16)
    grad_term = jnp.einsum("cfd,cfe->de", modulated, d_eps_b, preferred_element_type=jnp.float32)

    rows_dev = w_out.shape[0] // ways
    cols = grad_term.shape[1]
    n_dp = lax.axis_size("dp")
    total_clips = clips_dev * ways * n_dp * lax.axis_size("sec")
    extra = -(-total_clips // cols)
    extra = -(-extra // 8) * 8
    first_clip = (
        (lax.axis_index("sec") * n_dp + lax.axis_index("dp")) * ways + me
    ) * clips_dev
    columns = jnp.arange(extra * cols)
    slots = columns[None, :] == (first_clip + jnp.arange(clips_dev))[:, None]
    reward_rows = jnp.sum(jnp.where(slots, rewards[:, None], 0.0), axis=0).reshape(extra, cols)
    stacked = jnp.concatenate(
        [
            grad_term.reshape(ways, rows_dev, cols),
            jnp.broadcast_to(reward_rows[None], (ways, extra, cols)),
        ],
        axis=1,
    )
    seq_bits = ways.bit_length() - 1
    block = halving_sum(stacked, "seq", [jnp.float32] + [jnp.bfloat16] * (seq_bits - 1))
    if lax.axis_size("sec") * lax.axis_size("dp") == 16:
        block = quad_sum(quad_sum(block, ("sec", "dp"), 1, 3), ("sec", "dp"), 0, 2)
    else:
        block = doubling_sum(doubling_sum(block, "sec"), "dp")
    grad_w_out = block[:rows_dev]
    group_first = (lax.axis_index("sec") * n_dp + lax.axis_index("dp")) * ways * clips_dev
    all_rewards = block[rows_dev:].reshape(extra * cols)
    rewards_out = lax.dynamic_slice_in_dim(all_rewards, group_first, ways * clips_dev)
    return (rewards_out, grad_w_out, grad_hidden)


def solution(mesh):
    placed = (
        P(("sec", "dp", "seq"), None, None),
        P(("sec", "dp", "seq"), None),
        P(("sec", "dp", "seq"), None),
        P(("sec", "dp", "seq"), None, None),
        P(("sec", "dp", "seq")),
        P(),
        P(),
        P(),
        P(None, None, "seq"),
        P("seq", None),
        P("seq", None),
        P(),
        P(("sec", "dp")),
        P(("sec", "dp")),
    )
    return jax.shard_map(
        local,
        mesh=mesh,
        in_specs=placed,
        out_specs=(P(("sec", "dp")), P("seq", None), P(("sec", "dp", "seq"), None, None)),
        check_vma=False,
    )
```

```python
import jax
import jax.numpy as jnp
from jax import lax
from jax.sharding import PartitionSpec as P

D_REW = 2048
HEADS = 16
PROMPTS = 32


normalizing_sharpness = 10.0
epsilon = 1e-06
highest = lax.Precision.HIGHEST


def rotate(angle, first, second):
    cosine = jnp.cos(angle)
    sine_term = jnp.sin(angle)
    return (cosine * first + sine_term * second, cosine * second - sine_term * first)


def suffix(values):
    return jnp.sum(values, axis=1, keepdims=True) - jnp.cumsum(values, axis=1)


def local_path(motion):
    spin = motion[..., 0]
    theta = jnp.cumsum(spin, axis=1) - spin
    step_east, step_north = rotate(theta, motion[..., 1], motion[..., 2])
    path_east = jnp.cumsum(step_east, axis=1) - step_east
    path_north = jnp.cumsum(step_north, axis=1) - step_north
    return (theta, path_east, path_north)


def embed(motion, root_east, root_north, w_embed, root_rows):
    emb = jnp.einsum(
        "cfe,ed->cfd", motion.astype(jnp.bfloat16), w_embed, preferred_element_type=jnp.float32
    )
    emb = emb + root_east[..., None] * root_rows[0] + root_north[..., None] * root_rows[1]
    scale_rms = jnp.sqrt(jnp.mean(emb * emb, axis=-1, keepdims=True) + epsilon)
    return (emb / scale_rms, scale_rms)


def unit_rows(vectors):
    length = jnp.sqrt(jnp.sum(vectors * vectors, axis=-1, keepdims=True) + epsilon)
    return (vectors / length, length)


def norm_grad(grad, normed, scale_rms):
    return (grad - normed * jnp.mean(grad * normed, axis=-1, keepdims=True)) / scale_rms


def motion_grad(d_emb, normed_e, scale_rms, motion, theta, embed_rows, root_rows):
    d_unemb = norm_grad(d_emb, normed_e, scale_rms)
    d_embedded = jnp.einsum("cfd,ed->cfe", d_unemb, embed_rows, precision=highest)
    grad_east = suffix(jnp.sum(d_unemb * root_rows[0], axis=-1))
    grad_north = suffix(jnp.sum(d_unemb * root_rows[1], axis=-1))
    vel_east = motion[..., 1]
    vel_north = motion[..., 2]
    d_east, d_north = rotate(-theta, grad_east, grad_north)
    cosine = jnp.cos(theta)
    sine_term = jnp.sin(theta)
    d_theta = grad_east * (cosine * vel_north - sine_term * vel_east) - grad_north * (
        cosine * vel_east + sine_term * vel_north
    )
    d_spin = suffix(d_theta)
    return d_embedded.at[..., 0].add(d_spin).at[..., 1].add(d_east).at[..., 2].add(d_north)


def xor_pairs(size, bit):
    return [(i, i ^ bit) for i in range(size)]


def halving_sum(chunks, axis, wire_types):
    size = lax.axis_size(axis)
    me = lax.axis_index(axis)
    bits = size.bit_length() - 1
    assert 1 << bits == size
    buf = chunks.reshape((2,) * bits + chunks.shape[1:])
    for k in range(bits):
        mine = (me >> k) & 1
        keep = lax.dynamic_index_in_dim(buf, mine, axis=bits - 1 - k, keepdims=False)
        send = lax.dynamic_index_in_dim(buf, 1 - mine, axis=bits - 1 - k, keepdims=False)
        got = lax.ppermute(send.astype(wire_types[k]), axis, xor_pairs(size, 1 << k))
        buf = keep + got.astype(keep.dtype)
    return buf


def doubling_sum(value, axis):
    size = lax.axis_size(axis)
    bits = size.bit_length() - 1
    assert 1 << bits == size
    for k in range(bits):
        value = value + lax.ppermute(value, axis, xor_pairs(size, 1 << k))
    return value


def local(
    hidden,
    cond_shift,
    cond_scale,
    noisy,
    noise_level,
    w_out,
    w_embed,
    w_root,
    w_qkv,
    w_proj,
    text_table,
    text_ids,
    prompt_index,
    reward_weight,
):
    clips_dev = hidden.shape[0]
    ways = lax.axis_size("seq")
    me = lax.axis_index("seq")
    head_size = D_REW // HEADS
    root_rows = w_root.astype(jnp.float32)
    embed_rows = w_embed.astype(jnp.float32)

    vocab_rows = text_table.shape[0]
    local_ids = text_ids - me * vocab_rows
    inside = (local_ids >= 0) & (local_ids < vocab_rows)
    picked = jnp.take(text_table, jnp.clip(local_ids, 0, vocab_rows - 1), axis=0).astype(
        jnp.float32
    )
    text_part = jnp.sum(jnp.where(inside[..., None], picked, 0.0), axis=1)
    text_raw = doubling_sum(text_part, "seq")
    proj_size = w_proj.shape[0] * w_proj.shape[1]
    spare = -(-proj_size // (w_qkv.shape[0] * head_size))
    spare = -(-spare // 16) * 16
    proj_spare = jnp.pad(w_proj.reshape(-1), (0, w_qkv.shape[0] * spare * head_size - proj_size))
    w_ext = jnp.concatenate(
        [w_qkv, proj_spare.reshape(w_qkv.shape[0], spare, head_size)], axis=1
    )
    w_all = lax.all_gather(w_ext, "seq", axis=0)
    proj_gathered = (
        w_all[:, :, D_REW:, :]
        .reshape(ways, -1)[:, :proj_size]
        .reshape(ways * w_proj.shape[0], w_proj.shape[1])
    )

    hidden_f = hidden.astype(jnp.float32)
    centred = hidden_f - jnp.mean(hidden_f, axis=-1, keepdims=True)
    inv_std = lax.rsqrt(jnp.mean(centred * centred, axis=-1, keepdims=True) + epsilon)
    normed_h = centred * inv_std
    gain = 1.0 + cond_scale.astype(jnp.float32)[:, None, :]
    modulated = (normed_h * gain + cond_shift.astype(jnp.float32)[:, None, :]).astype(jnp.bfloat16)
    eps_pred = jnp.einsum("cfd,de->cfe", modulated, w_out, preferred_element_type=jnp.float32)
    level = noise_level[:, None, None]
    x_clean = noisy.astype(jnp.float32) - level * eps_pred
    theta, path_east, path_north = local_path(x_clean)
    normed_e, scale_rms = embed(x_clean, path_east, path_north, w_embed, root_rows)
    emb_b = normed_e.astype(jnp.bfloat16)
    emb_ext = jnp.pad(emb_b, ((0, 0), (0, 0), (0, w_all.shape[2] - D_REW)))
    w_all, proj_b, emb_ext, text_raw = lax.optimization_barrier(
        (w_all, proj_gathered, emb_ext, text_raw)
    )
    text_unit, text_len = unit_rows(text_raw)
    proj_rows = proj_b.astype(jnp.float32)
    projected = jnp.einsum(
        "cfd,hjdk->cfhjk",
        emb_ext,
        w_all,
        preferred_element_type=jnp.float32,
    )
    query_unit, query_len = unit_rows(projected[:, :, :, 0])
    key_unit, key_len = unit_rows(projected[:, :, :, 1])
    asking_vectors_group = query_unit.astype(jnp.bfloat16)
    lookup_vectors_group = key_unit.astype(jnp.bfloat16)
    value_b = projected[:, :, :, 2].astype(jnp.bfloat16)
    similarity_table = normalizing_sharpness * jnp.einsum(
        "cfhd,cghd->chfg",
        asking_vectors_group,
        lookup_vectors_group,
        preferred_element_type=jnp.float32,
    )
    expo = jnp.exp(similarity_table)
    focus_probabilities = expo / jnp.sum(expo, axis=-1, keepdims=True)
    attention_b = focus_probabilities.astype(jnp.bfloat16)
    column_mass = jnp.sum(attention_b, axis=2, dtype=jnp.float32)
    value_f = value_b.astype(jnp.float32)
    pooled = jnp.einsum("chg,cghd->chd", column_mass, value_f, precision=highest)
    pooled_b = pooled.astype(jnp.bfloat16).reshape(clips_dev, D_REW)
    motion_emb = jnp.dot(pooled_b, proj_b, preferred_element_type=jnp.float32)
    prompts = lax.dynamic_slice_in_dim(prompt_index, me * clips_dev, clips_dev)
    weights = lax.dynamic_slice_in_dim(reward_weight, me * clips_dev, clips_dev)
    choose = (prompts[:, None] == jnp.arange(PROMPTS)[None, :]).astype(jnp.float32)
    target = jnp.dot(choose, text_unit, precision=highest)
    emb_len = jnp.sqrt(jnp.sum(motion_emb * motion_emb, axis=-1) + epsilon)
    rewards = jnp.sum(motion_emb * target, axis=-1) / emb_len
    d_memb = (
        (-weights)[:, None]
        * (target - rewards[:, None] * motion_emb / emb_len[:, None])
        / emb_len[:, None]
    )
    d_pooled = jnp.dot(d_memb, proj_rows.T, precision=highest).reshape(
        clips_dev, HEADS, head_size
    )
    reduction_dimension = jnp.einsum("chd,cghd->chg", d_pooled, value_f, precision=highest)
    d_value = jnp.transpose(column_mass, (0, 2, 1))[..., None] * d_pooled[:, None]
    pairwise_dot_similarity = jnp.sum(
        focus_probabilities * reduction_dimension[:, :, None, :], axis=-1, keepdims=True
    )
    similarity_derivative = (
        normalizing_sharpness
        * focus_probabilities
        * (reduction_dimension[:, :, None, :] - pairwise_dot_similarity)
    ).astype(jnp.bfloat16)
    d_qu = jnp.einsum(
        "chfg,cghd->cfhd",
        similarity_derivative,
        lookup_vectors_group,
        preferred_element_type=jnp.float32,
    )
    d_ku = jnp.einsum(
        "chfg,cfhd->cghd",
        similarity_derivative,
        asking_vectors_group,
        preferred_element_type=jnp.float32,
    )
    d_query = (d_qu - query_unit * jnp.sum(query_unit * d_qu, axis=-1, keepdims=True)) / query_len
    d_key = (d_ku - key_unit * jnp.sum(key_unit * d_ku, axis=-1, keepdims=True)) / key_len
    d_proj = jnp.stack([d_query, d_key, d_value], axis=3).astype(jnp.bfloat16)
    d_emb = jnp.einsum("cfhjk,hjdk->cfd", d_proj, w_all, preferred_element_type=jnp.float32)
    d_emb = d_emb[..., :D_REW]
    d_motion = motion_grad(d_emb, normed_e, scale_rms, x_clean, theta, embed_rows, root_rows)
    d_eps_b = (-level * d_motion).astype(jnp.bfloat16)
    d_mod = jnp.einsum("cfe,de->cfd", d_eps_b, w_out, preferred_element_type=jnp.float32)
    d_norm = d_mod * gain
    grad_hidden = (
        inv_std
        * (
            d_norm
            - jnp.mean(d_norm, axis=-1, keepdims=True)
            - normed_h * jnp.mean(d_norm * normed_h, axis=-1, keepdims=True)
        )
    ).astype(jnp.bfloat16)
    grad_term = jnp.einsum("cfd,cfe->de", modulated, d_eps_b, preferred_element_type=jnp.float32)

    rows_dev = w_out.shape[0] // ways
    cols = grad_term.shape[1]
    n_dp = lax.axis_size("dp")
    total_clips = clips_dev * ways * n_dp * lax.axis_size("sec")
    extra = -(-total_clips // cols)
    extra = -(-extra // 8) * 8
    first_clip = (
        (lax.axis_index("sec") * n_dp + lax.axis_index("dp")) * ways + me
    ) * clips_dev
    columns = jnp.arange(extra * cols)
    slots = columns[None, :] == (first_clip + jnp.arange(clips_dev))[:, None]
    reward_rows = jnp.sum(jnp.where(slots, rewards[:, None], 0.0), axis=0).reshape(extra, cols)
    stacked = jnp.concatenate(
        [
            grad_term.reshape(ways, rows_dev, cols),
            jnp.broadcast_to(reward_rows[None], (ways, extra, cols)),
        ],
        axis=1,
    )
    seq_bits = ways.bit_length() - 1
    block = halving_sum(stacked, "seq", [jnp.float32] + [jnp.bfloat16] * (seq_bits - 1))
    block = doubling_sum(doubling_sum(block, "sec"), "dp")
    grad_w_out = block[:rows_dev]
    group_first = (lax.axis_index("sec") * n_dp + lax.axis_index("dp")) * ways * clips_dev
    all_rewards = block[rows_dev:].reshape(extra * cols)
    rewards_out = lax.dynamic_slice_in_dim(all_rewards, group_first, ways * clips_dev)
    return (rewards_out, grad_w_out, grad_hidden)


def solution(mesh):
    placed = (
        P(("sec", "dp", "seq"), None, None),
        P(("sec", "dp", "seq"), None),
        P(("sec", "dp", "seq"), None),
        P(("sec", "dp", "seq"), None, None),
        P(("sec", "dp", "seq")),
        P(),
        P(),
        P(),
        P(None, None, "seq"),
        P("seq", None),
        P("seq", None),
        P(),
        P(("sec", "dp")),
        P(("sec", "dp")),
    )
    return jax.shard_map(
        local,
        mesh=mesh,
        in_specs=placed,
        out_specs=(P(("sec", "dp")), P("seq", None), P(("sec", "dp", "seq"), None, None)),
        check_vma=False,
    )
```

```python
import jax
import jax.numpy as jnp
from jax import lax
from jax.sharding import PartitionSpec as P

D_REW = 2048
HEADS = 16
PROMPTS = 32


normalizing_sharpness = 10.0
epsilon = 1e-06
highest = lax.Precision.HIGHEST


def rotate(angle, first, second):
    cosine = jnp.cos(angle)
    sine_term = jnp.sin(angle)
    return (cosine * first + sine_term * second, cosine * second - sine_term * first)


def suffix(values):
    return jnp.sum(values, axis=1, keepdims=True) - jnp.cumsum(values, axis=1)


def local_path(motion):
    spin = motion[..., 0]
    theta = jnp.cumsum(spin, axis=1) - spin
    step_east, step_north = rotate(theta, motion[..., 1], motion[..., 2])
    path_east = jnp.cumsum(step_east, axis=1) - step_east
    path_north = jnp.cumsum(step_north, axis=1) - step_north
    return (theta, path_east, path_north)


def embed(motion, root_east, root_north, w_embed, root_rows):
    emb = jnp.einsum(
        "cfe,ed->cfd", motion.astype(jnp.bfloat16), w_embed, preferred_element_type=jnp.float32
    )
    emb = emb + root_east[..., None] * root_rows[0] + root_north[..., None] * root_rows[1]
    scale_rms = jnp.sqrt(jnp.mean(emb * emb, axis=-1, keepdims=True) + epsilon)
    return (emb / scale_rms, scale_rms)


def unit_rows(vectors):
    length = jnp.sqrt(jnp.sum(vectors * vectors, axis=-1, keepdims=True) + epsilon)
    return (vectors / length, length)


def norm_grad(grad, normed, scale_rms):
    return (grad - normed * jnp.mean(grad * normed, axis=-1, keepdims=True)) / scale_rms


def motion_grad(d_emb, normed_e, scale_rms, motion, theta, embed_rows, root_rows):
    d_unemb = norm_grad(d_emb, normed_e, scale_rms)
    d_embedded = jnp.einsum("cfd,ed->cfe", d_unemb, embed_rows, precision=highest)
    grad_east = suffix(jnp.sum(d_unemb * root_rows[0], axis=-1))
    grad_north = suffix(jnp.sum(d_unemb * root_rows[1], axis=-1))
    vel_east = motion[..., 1]
    vel_north = motion[..., 2]
    d_east, d_north = rotate(-theta, grad_east, grad_north)
    cosine = jnp.cos(theta)
    sine_term = jnp.sin(theta)
    d_theta = grad_east * (cosine * vel_north - sine_term * vel_east) - grad_north * (
        cosine * vel_east + sine_term * vel_north
    )
    d_spin = suffix(d_theta)
    return d_embedded.at[..., 0].add(d_spin).at[..., 1].add(d_east).at[..., 2].add(d_north)


def xor_pairs(size, bit):
    return [(i, i ^ bit) for i in range(size)]


def halving_sum(chunks, axis, wire_types, ride=None):
    size = lax.axis_size(axis)
    me = lax.axis_index(axis)
    bits = size.bit_length() - 1
    assert 1 << bits == size
    buf = chunks.reshape((2,) * bits + chunks.shape[1:])
    for k in range(bits):
        mine = (me >> k) & 1
        keep = lax.dynamic_index_in_dim(buf, mine, axis=bits - 1 - k, keepdims=False)
        send = lax.dynamic_index_in_dim(buf, 1 - mine, axis=bits - 1 - k, keepdims=False)
        got = lax.ppermute(send.astype(wire_types[k]), axis, xor_pairs(size, 1 << k))
        buf = keep + got.astype(keep.dtype)
        if k == 0:
            buf, ride = lax.optimization_barrier((buf, ride))
    return buf, ride


def doubling_sum(value, axis):
    size = lax.axis_size(axis)
    bits = size.bit_length() - 1
    assert 1 << bits == size
    for k in range(bits):
        value = value + lax.ppermute(value, axis, xor_pairs(size, 1 << k))
    return value


def local(
    hidden,
    cond_shift,
    cond_scale,
    noisy,
    noise_level,
    w_out,
    w_embed,
    w_root,
    w_qkv,
    w_proj,
    text_table,
    text_ids,
    prompt_index,
    reward_weight,
):
    clips_dev = hidden.shape[0]
    ways = lax.axis_size("seq")
    me = lax.axis_index("seq")
    head_size = D_REW // HEADS
    root_rows = w_root.astype(jnp.float32)
    embed_rows = w_embed.astype(jnp.float32)

    vocab_rows = text_table.shape[0]
    local_ids = text_ids - me * vocab_rows
    inside = (local_ids >= 0) & (local_ids < vocab_rows)
    picked = jnp.take(text_table, jnp.clip(local_ids, 0, vocab_rows - 1), axis=0).astype(
        jnp.float32
    )
    text_part = jnp.sum(jnp.where(inside[..., None], picked, 0.0), axis=1)
    text_raw = doubling_sum(text_part, "seq")
    w_all = lax.all_gather(w_qkv, "seq", axis=0)

    hidden_f = hidden.astype(jnp.float32)
    centred = hidden_f - jnp.mean(hidden_f, axis=-1, keepdims=True)
    inv_std = lax.rsqrt(jnp.mean(centred * centred, axis=-1, keepdims=True) + epsilon)
    normed_h = centred * inv_std
    gain = 1.0 + cond_scale.astype(jnp.float32)[:, None, :]
    modulated = (normed_h * gain + cond_shift.astype(jnp.float32)[:, None, :]).astype(jnp.bfloat16)
    eps_pred = jnp.einsum("cfd,de->cfe", modulated, w_out, preferred_element_type=jnp.float32)
    level = noise_level[:, None, None]
    x_clean = noisy.astype(jnp.float32) - level * eps_pred
    theta, path_east, path_north = local_path(x_clean)
    normed_e, scale_rms = embed(x_clean, path_east, path_north, w_embed, root_rows)
    w_all, proj_send, emb_b, text_raw, modulated_t = lax.optimization_barrier(
        (w_all, w_proj, normed_e.astype(jnp.bfloat16), text_raw, jnp.swapaxes(modulated, 1, 2))
    )
    text_unit, text_len = unit_rows(text_raw)
    proj_b = lax.all_gather(proj_send, "seq", axis=0, tiled=True)
    proj_rows = proj_b.astype(jnp.float32)
    projected = jnp.einsum(
        "cfd,hjdk->cfhjk",
        emb_b,
        w_all,
        preferred_element_type=jnp.float32,
    )
    query_unit, query_len = unit_rows(projected[:, :, :, 0])
    key_unit, key_len = unit_rows(projected[:, :, :, 1])
    asking_vectors_group = query_unit.astype(jnp.bfloat16)
    lookup_vectors_group = key_unit.astype(jnp.bfloat16)
    value_b = projected[:, :, :, 2].astype(jnp.bfloat16)
    similarity_table = normalizing_sharpness * jnp.einsum(
        "cfhd,cghd->chfg",
        asking_vectors_group,
        lookup_vectors_group,
        preferred_element_type=jnp.float32,
    )
    expo = jnp.exp(similarity_table)
    focus_probabilities = expo / jnp.sum(expo, axis=-1, keepdims=True)
    attention_b = focus_probabilities.astype(jnp.bfloat16)
    column_mass = jnp.sum(attention_b, axis=2, dtype=jnp.float32)
    value_f = value_b.astype(jnp.float32)
    pooled = jnp.einsum("chg,cghd->chd", column_mass, value_f, precision=highest)
    pooled_b = pooled.astype(jnp.bfloat16).reshape(clips_dev, D_REW)
    motion_emb = jnp.dot(pooled_b, proj_b, preferred_element_type=jnp.float32)
    prompts = lax.dynamic_slice_in_dim(prompt_index, me * clips_dev, clips_dev)
    weights = lax.dynamic_slice_in_dim(reward_weight, me * clips_dev, clips_dev)
    choose = (prompts[:, None] == jnp.arange(PROMPTS)[None, :]).astype(jnp.float32)
    target = jnp.dot(choose, text_unit, precision=highest)
    emb_len = jnp.sqrt(jnp.sum(motion_emb * motion_emb, axis=-1) + epsilon)
    rewards = jnp.sum(motion_emb * target, axis=-1) / emb_len
    d_memb = (
        (-weights)[:, None]
        * (target - rewards[:, None] * motion_emb / emb_len[:, None])
        / emb_len[:, None]
    )
    d_pooled = jnp.dot(d_memb, proj_rows.T, precision=highest).reshape(
        clips_dev, HEADS, head_size
    )
    reduction_dimension = jnp.einsum("chd,cghd->chg", d_pooled, value_f, precision=highest)
    d_value = jnp.transpose(column_mass, (0, 2, 1))[..., None] * d_pooled[:, None]
    pairwise_dot_similarity = jnp.sum(
        focus_probabilities * reduction_dimension[:, :, None, :], axis=-1, keepdims=True
    )
    similarity_derivative = (
        normalizing_sharpness
        * focus_probabilities
        * (reduction_dimension[:, :, None, :] - pairwise_dot_similarity)
    ).astype(jnp.bfloat16)
    d_qu = jnp.einsum(
        "chfg,cghd->cfhd",
        similarity_derivative,
        lookup_vectors_group,
        preferred_element_type=jnp.float32,
    )
    d_ku = jnp.einsum(
        "chfg,cfhd->cghd",
        similarity_derivative,
        asking_vectors_group,
        preferred_element_type=jnp.float32,
    )
    d_query = (d_qu - query_unit * jnp.sum(query_unit * d_qu, axis=-1, keepdims=True)) / query_len
    d_key = (d_ku - key_unit * jnp.sum(key_unit * d_ku, axis=-1, keepdims=True)) / key_len
    d_proj = jnp.stack([d_query, d_key, d_value], axis=3).astype(jnp.bfloat16)
    d_emb = jnp.einsum("cfhjk,hjdk->cfd", d_proj, w_all, preferred_element_type=jnp.float32)
    d_motion = motion_grad(d_emb, normed_e, scale_rms, x_clean, theta, embed_rows, root_rows)
    d_eps_b = (-level * d_motion).astype(jnp.bfloat16)
    grad_term = jnp.einsum(
        "cdf,cfe->de", modulated_t, d_eps_b, preferred_element_type=jnp.float32
    )

    rows_dev = w_out.shape[0] // ways
    cols = grad_term.shape[1]
    n_dp = lax.axis_size("dp")
    total_clips = clips_dev * ways * n_dp * lax.axis_size("sec")
    extra = -(-total_clips // cols)
    extra = -(-extra // 8) * 8
    first_clip = (
        (lax.axis_index("sec") * n_dp + lax.axis_index("dp")) * ways + me
    ) * clips_dev
    columns = jnp.arange(extra * cols)
    slots = columns[None, :] == (first_clip + jnp.arange(clips_dev))[:, None]
    reward_rows = jnp.sum(jnp.where(slots, rewards[:, None], 0.0), axis=0).reshape(extra, cols)
    stacked = jnp.concatenate(
        [
            grad_term.reshape(ways, rows_dev, cols),
            jnp.broadcast_to(reward_rows[None], (ways, extra, cols)),
        ],
        axis=1,
    )
    seq_bits = ways.bit_length() - 1
    block, d_eps_b = halving_sum(
        stacked, "seq", [jnp.float32] + [jnp.bfloat16] * (seq_bits - 1), ride=d_eps_b
    )
    d_mod = jnp.einsum("cfe,de->cfd", d_eps_b, w_out, preferred_element_type=jnp.float32)
    d_norm = d_mod * gain
    grad_hidden = (
        inv_std
        * (
            d_norm
            - jnp.mean(d_norm, axis=-1, keepdims=True)
            - normed_h * jnp.mean(d_norm * normed_h, axis=-1, keepdims=True)
        )
    ).astype(jnp.bfloat16)
    block = doubling_sum(doubling_sum(block, "sec"), "dp")
    grad_w_out = block[:rows_dev]
    group_first = (lax.axis_index("sec") * n_dp + lax.axis_index("dp")) * ways * clips_dev
    all_rewards = block[rows_dev:].reshape(extra * cols)
    rewards_out = lax.dynamic_slice_in_dim(all_rewards, group_first, ways * clips_dev)
    return (rewards_out, grad_w_out, grad_hidden)


def solution(mesh):
    placed = (
        P(("sec", "dp", "seq"), None, None),
        P(("sec", "dp", "seq"), None),
        P(("sec", "dp", "seq"), None),
        P(("sec", "dp", "seq"), None, None),
        P(("sec", "dp", "seq")),
        P(),
        P(),
        P(),
        P(None, None, "seq"),
        P("seq", None),
        P("seq", None),
        P(),
        P(("sec", "dp")),
        P(("sec", "dp")),
    )
    return jax.shard_map(
        local,
        mesh=mesh,
        in_specs=placed,
        out_specs=(P(("sec", "dp")), P("seq", None), P(("sec", "dp", "seq"), None, None)),
        check_vma=False,
    )
```

```python
import jax
import jax.numpy as jnp
from jax import lax
from jax.sharding import PartitionSpec as P

D_REW = 2048
HEADS = 16
PROMPTS = 32


normalizing_sharpness = 10.0
epsilon = 1e-06
highest = lax.Precision.HIGHEST


def rotate(angle, first, second):
    cosine = jnp.cos(angle)
    sine_term = jnp.sin(angle)
    return (cosine * first + sine_term * second, cosine * second - sine_term * first)


def suffix(values):
    return jnp.sum(values, axis=1, keepdims=True) - jnp.cumsum(values, axis=1)


def local_path(motion):
    spin = motion[..., 0]
    theta = jnp.cumsum(spin, axis=1) - spin
    step_east, step_north = rotate(theta, motion[..., 1], motion[..., 2])
    path_east = jnp.cumsum(step_east, axis=1) - step_east
    path_north = jnp.cumsum(step_north, axis=1) - step_north
    return (theta, path_east, path_north)


def embed(motion, root_east, root_north, w_embed, root_rows):
    emb = jnp.einsum(
        "cfe,ed->cfd", motion.astype(jnp.bfloat16), w_embed, preferred_element_type=jnp.float32
    )
    emb = emb + root_east[..., None] * root_rows[0] + root_north[..., None] * root_rows[1]
    scale_rms = jnp.sqrt(jnp.mean(emb * emb, axis=-1, keepdims=True) + epsilon)
    return (emb / scale_rms, scale_rms)


def unit_rows(vectors):
    length = jnp.sqrt(jnp.sum(vectors * vectors, axis=-1, keepdims=True) + epsilon)
    return (vectors / length, length)


def norm_grad(grad, normed, scale_rms):
    return (grad - normed * jnp.mean(grad * normed, axis=-1, keepdims=True)) / scale_rms


def motion_grad(d_emb, normed_e, scale_rms, motion, theta, embed_rows, root_rows):
    d_unemb = norm_grad(d_emb, normed_e, scale_rms)
    d_embedded = jnp.einsum("cfd,ed->cfe", d_unemb, embed_rows, precision=highest)
    grad_east = suffix(jnp.sum(d_unemb * root_rows[0], axis=-1))
    grad_north = suffix(jnp.sum(d_unemb * root_rows[1], axis=-1))
    vel_east = motion[..., 1]
    vel_north = motion[..., 2]
    d_east, d_north = rotate(-theta, grad_east, grad_north)
    cosine = jnp.cos(theta)
    sine_term = jnp.sin(theta)
    d_theta = grad_east * (cosine * vel_north - sine_term * vel_east) - grad_north * (
        cosine * vel_east + sine_term * vel_north
    )
    d_spin = suffix(d_theta)
    return d_embedded.at[..., 0].add(d_spin).at[..., 1].add(d_east).at[..., 2].add(d_north)


def xor_pairs(size, bit):
    return [(i, i ^ bit) for i in range(size)]


def halving_sum(chunks, axis, wire_types, ride=None):
    size = lax.axis_size(axis)
    me = lax.axis_index(axis)
    bits = size.bit_length() - 1
    assert 1 << bits == size
    buf = chunks.reshape((2,) * bits + chunks.shape[1:])
    for k in range(bits):
        mine = (me >> k) & 1
        keep = lax.dynamic_index_in_dim(buf, mine, axis=bits - 1 - k, keepdims=False)
        send = lax.dynamic_index_in_dim(buf, 1 - mine, axis=bits - 1 - k, keepdims=False)
        got = lax.ppermute(send.astype(wire_types[k]), axis, xor_pairs(size, 1 << k))
        buf = keep + got.astype(keep.dtype)
        if k == 0:
            buf, ride = lax.optimization_barrier((buf, ride))
    return buf, ride


def doubling_gather(value, axis):
    size = lax.axis_size(axis)
    me = lax.axis_index(axis)
    bits = size.bit_length() - 1
    assert 1 << bits == size
    held = value[None]
    for k in reversed(range(bits)):
        held = jnp.concatenate([held, lax.ppermute(held, axis, xor_pairs(size, 1 << k))], axis=0)
    wanted = jnp.arange(size) ^ me
    position = sum(((wanted >> k) & 1) << (bits - 1 - k) for k in range(bits))
    return jnp.take(held, position, axis=0)


def doubling_sum(value, axis):
    size = lax.axis_size(axis)
    bits = size.bit_length() - 1
    assert 1 << bits == size
    for k in range(bits):
        value = value + lax.ppermute(value, axis, xor_pairs(size, 1 << k))
    return value


def local(
    hidden,
    cond_shift,
    cond_scale,
    noisy,
    noise_level,
    w_out,
    w_embed,
    w_root,
    w_qkv,
    w_proj,
    text_table,
    text_ids,
    prompt_index,
    reward_weight,
):
    clips_dev = hidden.shape[0]
    ways = lax.axis_size("seq")
    me = lax.axis_index("seq")
    head_size = D_REW // HEADS
    root_rows = w_root.astype(jnp.float32)
    embed_rows = w_embed.astype(jnp.float32)

    vocab_rows = text_table.shape[0]
    local_ids = text_ids - me * vocab_rows
    inside = (local_ids >= 0) & (local_ids < vocab_rows)
    picked = jnp.take(text_table, jnp.clip(local_ids, 0, vocab_rows - 1), axis=0).astype(
        jnp.float32
    )
    text_part = jnp.sum(jnp.where(inside[..., None], picked, 0.0), axis=1)
    text_raw = doubling_sum(text_part, "seq")
    w_all = lax.all_gather(w_qkv, "seq", axis=0)

    hidden_f = hidden.astype(jnp.float32)
    centred = hidden_f - jnp.mean(hidden_f, axis=-1, keepdims=True)
    inv_std = lax.rsqrt(jnp.mean(centred * centred, axis=-1, keepdims=True) + epsilon)
    normed_h = centred * inv_std
    gain = 1.0 + cond_scale.astype(jnp.float32)[:, None, :]
    modulated = (normed_h * gain + cond_shift.astype(jnp.float32)[:, None, :]).astype(jnp.bfloat16)
    eps_pred = jnp.einsum("cfd,de->cfe", modulated, w_out, preferred_element_type=jnp.float32)
    level = noise_level[:, None, None]
    x_clean = noisy.astype(jnp.float32) - level * eps_pred
    theta, path_east, path_north = local_path(x_clean)
    normed_e, scale_rms = embed(x_clean, path_east, path_north, w_embed, root_rows)
    w_all, proj_send, emb_b, text_raw, modulated_t = lax.optimization_barrier(
        (w_all, w_proj, normed_e.astype(jnp.bfloat16), text_raw, jnp.swapaxes(modulated, 1, 2))
    )
    text_unit, text_len = unit_rows(text_raw)
    proj_b = doubling_gather(proj_send, "seq").reshape(ways * w_proj.shape[0], w_proj.shape[1])
    proj_rows = proj_b.astype(jnp.float32)
    projected = jnp.einsum(
        "cfd,hjdk->cfhjk",
        emb_b,
        w_all,
        preferred_element_type=jnp.float32,
    )
    query_unit, query_len = unit_rows(projected[:, :, :, 0])
    key_unit, key_len = unit_rows(projected[:, :, :, 1])
    asking_vectors_group = query_unit.astype(jnp.bfloat16)
    lookup_vectors_group = key_unit.astype(jnp.bfloat16)
    value_b = projected[:, :, :, 2].astype(jnp.bfloat16)
    similarity_table = normalizing_sharpness * jnp.einsum(
        "cfhd,cghd->chfg",
        asking_vectors_group,
        lookup_vectors_group,
        preferred_element_type=jnp.float32,
    )
    expo = jnp.exp(similarity_table)
    focus_probabilities = expo / jnp.sum(expo, axis=-1, keepdims=True)
    attention_b = focus_probabilities.astype(jnp.bfloat16)
    column_mass = jnp.sum(attention_b, axis=2, dtype=jnp.float32)
    value_f = value_b.astype(jnp.float32)
    pooled = jnp.einsum("chg,cghd->chd", column_mass, value_f, precision=highest)
    pooled_b = pooled.astype(jnp.bfloat16).reshape(clips_dev, D_REW)
    motion_emb = jnp.dot(pooled_b, proj_b, preferred_element_type=jnp.float32)
    prompts = lax.dynamic_slice_in_dim(prompt_index, me * clips_dev, clips_dev)
    weights = lax.dynamic_slice_in_dim(reward_weight, me * clips_dev, clips_dev)
    choose = (prompts[:, None] == jnp.arange(PROMPTS)[None, :]).astype(jnp.float32)
    target = jnp.dot(choose, text_unit, precision=highest)
    emb_len = jnp.sqrt(jnp.sum(motion_emb * motion_emb, axis=-1) + epsilon)
    rewards = jnp.sum(motion_emb * target, axis=-1) / emb_len
    d_memb = (
        (-weights)[:, None]
        * (target - rewards[:, None] * motion_emb / emb_len[:, None])
        / emb_len[:, None]
    )
    d_pooled = jnp.dot(d_memb, proj_rows.T, precision=highest).reshape(
        clips_dev, HEADS, head_size
    )
    reduction_dimension = jnp.einsum("chd,cghd->chg", d_pooled, value_f, precision=highest)
    d_value = jnp.transpose(column_mass, (0, 2, 1))[..., None] * d_pooled[:, None]
    pairwise_dot_similarity = jnp.sum(
        focus_probabilities * reduction_dimension[:, :, None, :], axis=-1, keepdims=True
    )
    similarity_derivative = (
        normalizing_sharpness
        * focus_probabilities
        * (reduction_dimension[:, :, None, :] - pairwise_dot_similarity)
    ).astype(jnp.bfloat16)
    d_qu = jnp.einsum(
        "chfg,cghd->cfhd",
        similarity_derivative,
        lookup_vectors_group,
        preferred_element_type=jnp.float32,
    )
    d_ku = jnp.einsum(
        "chfg,cfhd->cghd",
        similarity_derivative,
        asking_vectors_group,
        preferred_element_type=jnp.float32,
    )
    d_query = (d_qu - query_unit * jnp.sum(query_unit * d_qu, axis=-1, keepdims=True)) / query_len
    d_key = (d_ku - key_unit * jnp.sum(key_unit * d_ku, axis=-1, keepdims=True)) / key_len
    d_proj = jnp.stack([d_query, d_key, d_value], axis=3).astype(jnp.bfloat16)
    d_emb = jnp.einsum("cfhjk,hjdk->cfd", d_proj, w_all, preferred_element_type=jnp.float32)
    d_motion = motion_grad(d_emb, normed_e, scale_rms, x_clean, theta, embed_rows, root_rows)
    d_eps_b = (-level * d_motion).astype(jnp.bfloat16)
    grad_term = jnp.einsum(
        "cdf,cfe->de", modulated_t, d_eps_b, preferred_element_type=jnp.float32
    )

    rows_dev = w_out.shape[0] // ways
    cols = grad_term.shape[1]
    n_dp = lax.axis_size("dp")
    total_clips = clips_dev * ways * n_dp * lax.axis_size("sec")
    extra = -(-total_clips // cols)
    extra = -(-extra // 8) * 8
    first_clip = (
        (lax.axis_index("sec") * n_dp + lax.axis_index("dp")) * ways + me
    ) * clips_dev
    columns = jnp.arange(extra * cols)
    slots = columns[None, :] == (first_clip + jnp.arange(clips_dev))[:, None]
    reward_rows = jnp.sum(jnp.where(slots, rewards[:, None], 0.0), axis=0).reshape(extra, cols)
    stacked = jnp.concatenate(
        [
            grad_term.reshape(ways, rows_dev, cols),
            jnp.broadcast_to(reward_rows[None], (ways, extra, cols)),
        ],
        axis=1,
    )
    seq_bits = ways.bit_length() - 1
    block, d_eps_b = halving_sum(
        stacked, "seq", [jnp.float32] + [jnp.bfloat16] * (seq_bits - 1), ride=d_eps_b
    )
    d_mod = jnp.einsum("cfe,de->cfd", d_eps_b, w_out, preferred_element_type=jnp.float32)
    d_norm = d_mod * gain
    grad_hidden = (
        inv_std
        * (
            d_norm
            - jnp.mean(d_norm, axis=-1, keepdims=True)
            - normed_h * jnp.mean(d_norm * normed_h, axis=-1, keepdims=True)
        )
    ).astype(jnp.bfloat16)
    block = doubling_sum(doubling_sum(block, "sec"), "dp")
    grad_w_out = block[:rows_dev]
    group_first = (lax.axis_index("sec") * n_dp + lax.axis_index("dp")) * ways * clips_dev
    all_rewards = block[rows_dev:].reshape(extra * cols)
    rewards_out = lax.dynamic_slice_in_dim(all_rewards, group_first, ways * clips_dev)
    return (rewards_out, grad_w_out, grad_hidden)


def solution(mesh):
    placed = (
        P(("sec", "dp", "seq"), None, None),
        P(("sec", "dp", "seq"), None),
        P(("sec", "dp", "seq"), None),
        P(("sec", "dp", "seq"), None, None),
        P(("sec", "dp", "seq")),
        P(),
        P(),
        P(),
        P(None, None, "seq"),
        P("seq", None),
        P("seq", None),
        P(),
        P(("sec", "dp")),
        P(("sec", "dp")),
    )
    return jax.shard_map(
        local,
        mesh=mesh,
        in_specs=placed,
        out_specs=(P(("sec", "dp")), P("seq", None), P(("sec", "dp", "seq"), None, None)),
        check_vma=False,
    )
```

```python
import jax
import jax.numpy as jnp
from jax import lax
from jax.sharding import PartitionSpec as P

D_REW = 2048
HEADS = 16
PROMPTS = 32


normalizing_sharpness = 10.0
epsilon = 1e-06
highest = lax.Precision.HIGHEST


def rotate(angle, first, second):
    cosine = jnp.cos(angle)
    sine_term = jnp.sin(angle)
    return (cosine * first + sine_term * second, cosine * second - sine_term * first)


def suffix(values):
    return jnp.sum(values, axis=1, keepdims=True) - jnp.cumsum(values, axis=1)


def local_path(motion):
    spin = motion[..., 0]
    theta = jnp.cumsum(spin, axis=1) - spin
    step_east, step_north = rotate(theta, motion[..., 1], motion[..., 2])
    path_east = jnp.cumsum(step_east, axis=1) - step_east
    path_north = jnp.cumsum(step_north, axis=1) - step_north
    return (theta, path_east, path_north)


def embed(motion, root_east, root_north, w_embed, root_rows):
    emb = jnp.einsum(
        "cfe,ed->cfd", motion.astype(jnp.bfloat16), w_embed, preferred_element_type=jnp.float32
    )
    emb = emb + root_east[..., None] * root_rows[0] + root_north[..., None] * root_rows[1]
    scale_rms = jnp.sqrt(jnp.mean(emb * emb, axis=-1, keepdims=True) + epsilon)
    return (emb / scale_rms, scale_rms)


def unit_rows(vectors):
    length = jnp.sqrt(jnp.sum(vectors * vectors, axis=-1, keepdims=True) + epsilon)
    return (vectors / length, length)


def norm_grad(grad, normed, scale_rms):
    return (grad - normed * jnp.mean(grad * normed, axis=-1, keepdims=True)) / scale_rms


def motion_grad(d_emb, normed_e, scale_rms, motion, theta, embed_rows, root_rows):
    d_unemb = norm_grad(d_emb, normed_e, scale_rms)
    d_embedded = jnp.einsum("cfd,ed->cfe", d_unemb, embed_rows, precision=highest)
    grad_east = suffix(jnp.sum(d_unemb * root_rows[0], axis=-1))
    grad_north = suffix(jnp.sum(d_unemb * root_rows[1], axis=-1))
    vel_east = motion[..., 1]
    vel_north = motion[..., 2]
    d_east, d_north = rotate(-theta, grad_east, grad_north)
    cosine = jnp.cos(theta)
    sine_term = jnp.sin(theta)
    d_theta = grad_east * (cosine * vel_north - sine_term * vel_east) - grad_north * (
        cosine * vel_east + sine_term * vel_north
    )
    d_spin = suffix(d_theta)
    return d_embedded.at[..., 0].add(d_spin).at[..., 1].add(d_east).at[..., 2].add(d_north)


def xor_pairs(size, bit):
    return [(i, i ^ bit) for i in range(size)]


def halving_sum(chunks, axis, wire_types, ride=None):
    size = lax.axis_size(axis)
    me = lax.axis_index(axis)
    bits = size.bit_length() - 1
    assert 1 << bits == size
    buf = chunks.reshape((2,) * bits + chunks.shape[1:])
    for k in range(bits):
        mine = (me >> k) & 1
        keep = lax.dynamic_index_in_dim(buf, mine, axis=bits - 1 - k, keepdims=False)
        send = lax.dynamic_index_in_dim(buf, 1 - mine, axis=bits - 1 - k, keepdims=False)
        got = lax.ppermute(send.astype(wire_types[k]), axis, xor_pairs(size, 1 << k))
        buf = keep + got.astype(keep.dtype)
        if k == 0:
            buf, ride = lax.optimization_barrier((buf, ride))
    return buf, ride


def doubling_sum(value, axis, wire_type=None):
    size = lax.axis_size(axis)
    bits = size.bit_length() - 1
    assert 1 << bits == size
    for k in range(bits):
        if wire_type is None:
            value = value + lax.ppermute(value, axis, xor_pairs(size, 1 << k))
        else:
            sent = value.astype(wire_type)
            got = lax.ppermute(sent, axis, xor_pairs(size, 1 << k))
            value = sent.astype(value.dtype) + got.astype(value.dtype)
    return value


def local(
    hidden,
    cond_shift,
    cond_scale,
    noisy,
    noise_level,
    w_out,
    w_embed,
    w_root,
    w_qkv,
    w_proj,
    text_table,
    text_ids,
    prompt_index,
    reward_weight,
):
    clips_dev = hidden.shape[0]
    ways = lax.axis_size("seq")
    me = lax.axis_index("seq")
    head_size = D_REW // HEADS
    root_rows = w_root.astype(jnp.float32)
    embed_rows = w_embed.astype(jnp.float32)

    vocab_rows = text_table.shape[0]
    local_ids = text_ids - me * vocab_rows
    inside = (local_ids >= 0) & (local_ids < vocab_rows)
    picked = jnp.take(text_table, jnp.clip(local_ids, 0, vocab_rows - 1), axis=0).astype(
        jnp.float32
    )
    text_part = jnp.sum(jnp.where(inside[..., None], picked, 0.0), axis=1)
    text_raw = doubling_sum(text_part, "seq")
    w_all = lax.all_gather(w_qkv, "seq", axis=0)

    hidden_f = hidden.astype(jnp.float32)
    centred = hidden_f - jnp.mean(hidden_f, axis=-1, keepdims=True)
    inv_std = lax.rsqrt(jnp.mean(centred * centred, axis=-1, keepdims=True) + epsilon)
    normed_h = centred * inv_std
    gain = 1.0 + cond_scale.astype(jnp.float32)[:, None, :]
    modulated = (normed_h * gain + cond_shift.astype(jnp.float32)[:, None, :]).astype(jnp.bfloat16)
    eps_pred = jnp.einsum("cfd,de->cfe", modulated, w_out, preferred_element_type=jnp.float32)
    level = noise_level[:, None, None]
    x_clean = noisy.astype(jnp.float32) - level * eps_pred
    theta, path_east, path_north = local_path(x_clean)
    normed_e, scale_rms = embed(x_clean, path_east, path_north, w_embed, root_rows)
    w_all, proj_send, emb_b, text_raw, modulated_t = lax.optimization_barrier(
        (w_all, w_proj, normed_e.astype(jnp.bfloat16), text_raw, jnp.swapaxes(modulated, 1, 2))
    )
    text_unit, text_len = unit_rows(text_raw)
    proj_b = lax.all_gather(proj_send, "seq", axis=0, tiled=True)
    proj_rows = proj_b.astype(jnp.float32)
    projected = jnp.einsum(
        "cfd,hjdk->cfhjk",
        emb_b,
        w_all,
        preferred_element_type=jnp.float32,
    )
    query_unit, query_len = unit_rows(projected[:, :, :, 0])
    key_unit, key_len = unit_rows(projected[:, :, :, 1])
    asking_vectors_group = query_unit.astype(jnp.bfloat16)
    lookup_vectors_group = key_unit.astype(jnp.bfloat16)
    value_b = projected[:, :, :, 2].astype(jnp.bfloat16)
    similarity_table = normalizing_sharpness * jnp.einsum(
        "cfhd,cghd->chfg",
        asking_vectors_group,
        lookup_vectors_group,
        preferred_element_type=jnp.float32,
    )
    expo = jnp.exp(similarity_table)
    focus_probabilities = expo / jnp.sum(expo, axis=-1, keepdims=True)
    attention_b = focus_probabilities.astype(jnp.bfloat16)
    column_mass = jnp.sum(attention_b, axis=2, dtype=jnp.float32)
    value_f = value_b.astype(jnp.float32)
    pooled = jnp.einsum("chg,cghd->chd", column_mass, value_f, precision=highest)
    pooled_b = pooled.astype(jnp.bfloat16).reshape(clips_dev, D_REW)
    motion_emb = jnp.dot(pooled_b, proj_b, preferred_element_type=jnp.float32)
    prompts = lax.dynamic_slice_in_dim(prompt_index, me * clips_dev, clips_dev)
    weights = lax.dynamic_slice_in_dim(reward_weight, me * clips_dev, clips_dev)
    choose = (prompts[:, None] == jnp.arange(PROMPTS)[None, :]).astype(jnp.float32)
    target = jnp.dot(choose, text_unit, precision=highest)
    emb_len = jnp.sqrt(jnp.sum(motion_emb * motion_emb, axis=-1) + epsilon)
    rewards = jnp.sum(motion_emb * target, axis=-1) / emb_len
    d_memb = (
        (-weights)[:, None]
        * (target - rewards[:, None] * motion_emb / emb_len[:, None])
        / emb_len[:, None]
    )
    d_pooled = jnp.dot(d_memb, proj_rows.T, precision=highest).reshape(
        clips_dev, HEADS, head_size
    )
    reduction_dimension = jnp.einsum("chd,cghd->chg", d_pooled, value_f, precision=highest)
    d_value = jnp.transpose(column_mass, (0, 2, 1))[..., None] * d_pooled[:, None]
    pairwise_dot_similarity = jnp.sum(
        focus_probabilities * reduction_dimension[:, :, None, :], axis=-1, keepdims=True
    )
    similarity_derivative = (
        normalizing_sharpness
        * focus_probabilities
        * (reduction_dimension[:, :, None, :] - pairwise_dot_similarity)
    ).astype(jnp.bfloat16)
    d_qu = jnp.einsum(
        "chfg,cghd->cfhd",
        similarity_derivative,
        lookup_vectors_group,
        preferred_element_type=jnp.float32,
    )
    d_ku = jnp.einsum(
        "chfg,cfhd->cghd",
        similarity_derivative,
        asking_vectors_group,
        preferred_element_type=jnp.float32,
    )
    d_query = (d_qu - query_unit * jnp.sum(query_unit * d_qu, axis=-1, keepdims=True)) / query_len
    d_key = (d_ku - key_unit * jnp.sum(key_unit * d_ku, axis=-1, keepdims=True)) / key_len
    d_proj = jnp.stack([d_query, d_key, d_value], axis=3).astype(jnp.bfloat16)
    d_emb = jnp.einsum("cfhjk,hjdk->cfd", d_proj, w_all, preferred_element_type=jnp.float32)
    d_motion = motion_grad(d_emb, normed_e, scale_rms, x_clean, theta, embed_rows, root_rows)
    d_eps_b = (-level * d_motion).astype(jnp.bfloat16)
    grad_term = jnp.einsum(
        "cdf,cfe->de", modulated_t, d_eps_b, preferred_element_type=jnp.float32
    )

    rows_dev = w_out.shape[0] // ways
    cols = grad_term.shape[1]
    n_dp = lax.axis_size("dp")
    total_clips = clips_dev * ways * n_dp * lax.axis_size("sec")
    extra = -(-total_clips // cols)
    extra = -(-extra // 8) * 8
    first_clip = (
        (lax.axis_index("sec") * n_dp + lax.axis_index("dp")) * ways + me
    ) * clips_dev
    columns = jnp.arange(extra * cols)
    slots = columns[None, :] == (first_clip + jnp.arange(clips_dev))[:, None]
    reward_rows = jnp.sum(jnp.where(slots, rewards[:, None], 0.0), axis=0).reshape(extra, cols)
    stacked = jnp.concatenate(
        [
            grad_term.reshape(ways, rows_dev, cols),
            jnp.broadcast_to(reward_rows[None], (ways, extra, cols)),
        ],
        axis=1,
    )
    seq_bits = ways.bit_length() - 1
    block, d_eps_b = halving_sum(
        stacked, "seq", [jnp.float32] + [jnp.bfloat16] * (seq_bits - 1), ride=d_eps_b
    )
    d_mod = jnp.einsum("cfe,de->cfd", d_eps_b, w_out, preferred_element_type=jnp.float32)
    d_norm = d_mod * gain
    grad_hidden = (
        inv_std
        * (
            d_norm
            - jnp.mean(d_norm, axis=-1, keepdims=True)
            - normed_h * jnp.mean(d_norm * normed_h, axis=-1, keepdims=True)
        )
    ).astype(jnp.bfloat16)
    block = doubling_sum(doubling_sum(block, "sec", jnp.bfloat16), "dp", jnp.bfloat16)
    grad_w_out = block[:rows_dev]
    group_first = (lax.axis_index("sec") * n_dp + lax.axis_index("dp")) * ways * clips_dev
    all_rewards = block[rows_dev:].reshape(extra * cols)
    rewards_out = lax.dynamic_slice_in_dim(all_rewards, group_first, ways * clips_dev)
    return (rewards_out, grad_w_out, grad_hidden)


def solution(mesh):
    placed = (
        P(("sec", "dp", "seq"), None, None),
        P(("sec", "dp", "seq"), None),
        P(("sec", "dp", "seq"), None),
        P(("sec", "dp", "seq"), None, None),
        P(("sec", "dp", "seq")),
        P(),
        P(),
        P(),
        P(None, None, "seq"),
        P("seq", None),
        P("seq", None),
        P(),
        P(("sec", "dp")),
        P(("sec", "dp")),
    )
    return jax.shard_map(
        local,
        mesh=mesh,
        in_specs=placed,
        out_specs=(P(("sec", "dp")), P("seq", None), P(("sec", "dp", "seq"), None, None)),
        check_vma=False,
    )
```

```python
import jax
import jax.numpy as jnp
from jax import lax
from jax.sharding import PartitionSpec as P

D_REW = 2048
HEADS = 16
PROMPTS = 32


normalizing_sharpness = 10.0
epsilon = 1e-06
highest = lax.Precision.HIGHEST


def rotate(angle, first, second):
    cosine = jnp.cos(angle)
    sine_term = jnp.sin(angle)
    return (cosine * first + sine_term * second, cosine * second - sine_term * first)


def suffix(values):
    return jnp.sum(values, axis=1, keepdims=True) - jnp.cumsum(values, axis=1)


def local_path(motion):
    spin = motion[..., 0]
    theta = jnp.cumsum(spin, axis=1) - spin
    step_east, step_north = rotate(theta, motion[..., 1], motion[..., 2])
    path_east = jnp.cumsum(step_east, axis=1) - step_east
    path_north = jnp.cumsum(step_north, axis=1) - step_north
    return (theta, path_east, path_north)


def embed(motion, root_east, root_north, w_embed, root_rows):
    emb = jnp.einsum(
        "cfe,ed->cfd", motion.astype(jnp.bfloat16), w_embed, preferred_element_type=jnp.float32
    )
    emb = emb + root_east[..., None] * root_rows[0] + root_north[..., None] * root_rows[1]
    scale_rms = jnp.sqrt(jnp.mean(emb * emb, axis=-1, keepdims=True) + epsilon)
    return (emb / scale_rms, scale_rms)


def unit_rows(vectors):
    length = jnp.sqrt(jnp.sum(vectors * vectors, axis=-1, keepdims=True) + epsilon)
    return (vectors / length, length)


def bf16_parts(values):
    high = lax.reduce_precision(values, exponent_bits=8, mantissa_bits=7)
    rest = values - high
    middle = lax.reduce_precision(rest, exponent_bits=8, mantissa_bits=7)
    return jnp.stack([high, middle, rest - middle]).astype(jnp.bfloat16)


def norm_grad(grad, normed, scale_rms):
    return (grad - normed * jnp.mean(grad * normed, axis=-1, keepdims=True)) / scale_rms


def motion_grad(d_emb, normed_e, scale_rms, motion, theta, w_embed, root_rows):
    d_unemb = norm_grad(d_emb, normed_e, scale_rms)
    d_embedded = jnp.sum(
        jnp.einsum("pcfd,ed->pcfe", bf16_parts(d_unemb), w_embed, preferred_element_type=jnp.float32),
        axis=0,
    )
    grad_east = suffix(jnp.sum(d_unemb * root_rows[0], axis=-1))
    grad_north = suffix(jnp.sum(d_unemb * root_rows[1], axis=-1))
    vel_east = motion[..., 1]
    vel_north = motion[..., 2]
    d_east, d_north = rotate(-theta, grad_east, grad_north)
    cosine = jnp.cos(theta)
    sine_term = jnp.sin(theta)
    d_theta = grad_east * (cosine * vel_north - sine_term * vel_east) - grad_north * (
        cosine * vel_east + sine_term * vel_north
    )
    d_spin = suffix(d_theta)
    return d_embedded.at[..., 0].add(d_spin).at[..., 1].add(d_east).at[..., 2].add(d_north)


def xor_pairs(size, bit):
    return [(i, i ^ bit) for i in range(size)]


def halving_sum(chunks, axis, wire_types, ride=None):
    size = lax.axis_size(axis)
    me = lax.axis_index(axis)
    bits = size.bit_length() - 1
    assert 1 << bits == size
    buf = chunks.reshape((2,) * bits + chunks.shape[1:])
    for k in range(bits):
        mine = (me >> k) & 1
        keep = lax.dynamic_index_in_dim(buf, mine, axis=bits - 1 - k, keepdims=False)
        send = lax.dynamic_index_in_dim(buf, 1 - mine, axis=bits - 1 - k, keepdims=False)
        got = lax.ppermute(send.astype(wire_types[k]), axis, xor_pairs(size, 1 << k))
        buf = keep + got.astype(keep.dtype)
        if k == 0:
            buf, ride = lax.optimization_barrier((buf, ride))
    return buf, ride


def doubling_sum(value, axis, wire_type=None):
    size = lax.axis_size(axis)
    bits = size.bit_length() - 1
    assert 1 << bits == size
    for k in range(bits):
        if wire_type is None:
            value = value + lax.ppermute(value, axis, xor_pairs(size, 1 << k))
        else:
            sent = value.astype(wire_type)
            got = lax.ppermute(sent, axis, xor_pairs(size, 1 << k))
            value = sent.astype(value.dtype) + got.astype(value.dtype)
    return value


def local(
    hidden,
    cond_shift,
    cond_scale,
    noisy,
    noise_level,
    w_out,
    w_embed,
    w_root,
    w_qkv,
    w_proj,
    text_table,
    text_ids,
    prompt_index,
    reward_weight,
):
    clips_dev = hidden.shape[0]
    ways = lax.axis_size("seq")
    me = lax.axis_index("seq")
    head_size = D_REW // HEADS
    root_rows = w_root.astype(jnp.float32)

    vocab_rows = text_table.shape[0]
    local_ids = text_ids - me * vocab_rows
    inside = (local_ids >= 0) & (local_ids < vocab_rows)
    picked = jnp.take(text_table, jnp.clip(local_ids, 0, vocab_rows - 1), axis=0).astype(
        jnp.float32
    )
    text_part = jnp.sum(jnp.where(inside[..., None], picked, 0.0), axis=1)
    text_raw = doubling_sum(text_part, "seq")
    w_all = lax.all_gather(w_qkv, "seq", axis=0)

    hidden_f = hidden.astype(jnp.float32)
    centred = hidden_f - jnp.mean(hidden_f, axis=-1, keepdims=True)
    inv_std = lax.rsqrt(jnp.mean(centred * centred, axis=-1, keepdims=True) + epsilon)
    normed_h = centred * inv_std
    gain = 1.0 + cond_scale.astype(jnp.float32)[:, None, :]
    modulated = (normed_h * gain + cond_shift.astype(jnp.float32)[:, None, :]).astype(jnp.bfloat16)
    eps_pred = jnp.einsum("cfd,de->cfe", modulated, w_out, preferred_element_type=jnp.float32)
    level = noise_level[:, None, None]
    x_clean = noisy.astype(jnp.float32) - level * eps_pred
    theta, path_east, path_north = local_path(x_clean)
    normed_e, scale_rms = embed(x_clean, path_east, path_north, w_embed, root_rows)
    w_all, proj_send, emb_b, text_raw, modulated_t = lax.optimization_barrier(
        (w_all, w_proj, normed_e.astype(jnp.bfloat16), text_raw, jnp.swapaxes(modulated, 1, 2))
    )
    text_unit, text_len = unit_rows(text_raw)
    proj_b = lax.all_gather(proj_send, "seq", axis=0, tiled=True)
    projected = jnp.einsum(
        "cfd,hjdk->cfhjk",
        emb_b,
        w_all,
        preferred_element_type=jnp.float32,
    )
    query_unit, query_len = unit_rows(projected[:, :, :, 0])
    key_unit, key_len = unit_rows(projected[:, :, :, 1])
    asking_vectors_group = query_unit.astype(jnp.bfloat16)
    lookup_vectors_group = key_unit.astype(jnp.bfloat16)
    value_b = projected[:, :, :, 2].astype(jnp.bfloat16)
    similarity_table = normalizing_sharpness * jnp.einsum(
        "cfhd,cghd->chfg",
        asking_vectors_group,
        lookup_vectors_group,
        preferred_element_type=jnp.float32,
    )
    expo = jnp.exp(similarity_table)
    focus_probabilities = expo / jnp.sum(expo, axis=-1, keepdims=True)
    attention_b = focus_probabilities.astype(jnp.bfloat16)
    column_mass = jnp.sum(attention_b, axis=2, dtype=jnp.float32)
    value_f = value_b.astype(jnp.float32)
    pooled = jnp.einsum("chg,cghd->chd", column_mass, value_f, precision=highest)
    pooled_b = pooled.astype(jnp.bfloat16).reshape(clips_dev, D_REW)
    motion_emb = jnp.dot(pooled_b, proj_b, preferred_element_type=jnp.float32)
    prompts = lax.dynamic_slice_in_dim(prompt_index, me * clips_dev, clips_dev)
    weights = lax.dynamic_slice_in_dim(reward_weight, me * clips_dev, clips_dev)
    choose = (prompts[:, None] == jnp.arange(PROMPTS)[None, :]).astype(jnp.float32)
    target = jnp.dot(choose, text_unit, precision=highest)
    emb_len = jnp.sqrt(jnp.sum(motion_emb * motion_emb, axis=-1) + epsilon)
    rewards = jnp.sum(motion_emb * target, axis=-1) / emb_len
    d_memb = (
        (-weights)[:, None]
        * (target - rewards[:, None] * motion_emb / emb_len[:, None])
        / emb_len[:, None]
    )
    d_pooled = jnp.sum(
        jnp.einsum("pcn,rn->pcr", bf16_parts(d_memb), proj_b, preferred_element_type=jnp.float32),
        axis=0,
    ).reshape(clips_dev, HEADS, head_size)
    reduction_dimension = jnp.einsum("chd,cghd->chg", d_pooled, value_f, precision=highest)
    d_value = jnp.transpose(column_mass, (0, 2, 1))[..., None] * d_pooled[:, None]
    pairwise_dot_similarity = jnp.sum(
        focus_probabilities * reduction_dimension[:, :, None, :], axis=-1, keepdims=True
    )
    similarity_derivative = (
        normalizing_sharpness
        * focus_probabilities
        * (reduction_dimension[:, :, None, :] - pairwise_dot_similarity)
    ).astype(jnp.bfloat16)
    d_qu = jnp.einsum(
        "chfg,cghd->cfhd",
        similarity_derivative,
        lookup_vectors_group,
        preferred_element_type=jnp.float32,
    )
    d_ku = jnp.einsum(
        "chfg,cfhd->cghd",
        similarity_derivative,
        asking_vectors_group,
        preferred_element_type=jnp.float32,
    )
    d_query = (d_qu - query_unit * jnp.sum(query_unit * d_qu, axis=-1, keepdims=True)) / query_len
    d_key = (d_ku - key_unit * jnp.sum(key_unit * d_ku, axis=-1, keepdims=True)) / key_len
    d_proj = jnp.stack([d_query, d_key, d_value], axis=3).astype(jnp.bfloat16)
    d_emb = jnp.einsum("cfhjk,hjdk->cfd", d_proj, w_all, preferred_element_type=jnp.float32)
    d_motion = motion_grad(d_emb, normed_e, scale_rms, x_clean, theta, w_embed, root_rows)
    d_eps_b = (-level * d_motion).astype(jnp.bfloat16)
    grad_term = jnp.einsum(
        "cdf,cfe->de", modulated_t, d_eps_b, preferred_element_type=jnp.float32
    )

    rows_dev = w_out.shape[0] // ways
    cols = grad_term.shape[1]
    n_dp = lax.axis_size("dp")
    total_clips = clips_dev * ways * n_dp * lax.axis_size("sec")
    extra = -(-total_clips // cols)
    extra = -(-extra // 8) * 8
    first_clip = (
        (lax.axis_index("sec") * n_dp + lax.axis_index("dp")) * ways + me
    ) * clips_dev
    columns = jnp.arange(extra * cols)
    slots = columns[None, :] == (first_clip + jnp.arange(clips_dev))[:, None]
    reward_rows = jnp.sum(jnp.where(slots, rewards[:, None], 0.0), axis=0).reshape(extra, cols)
    stacked = jnp.concatenate(
        [
            grad_term.reshape(ways, rows_dev, cols),
            jnp.broadcast_to(reward_rows[None], (ways, extra, cols)),
        ],
        axis=1,
    )
    seq_bits = ways.bit_length() - 1
    block, d_eps_b = halving_sum(
        stacked, "seq", [jnp.float32] + [jnp.bfloat16] * (seq_bits - 1), ride=d_eps_b
    )
    d_mod = jnp.einsum("cfe,de->cfd", d_eps_b, w_out, preferred_element_type=jnp.float32)
    d_norm = d_mod * gain
    grad_hidden = (
        inv_std
        * (
            d_norm
            - jnp.mean(d_norm, axis=-1, keepdims=True)
            - normed_h * jnp.mean(d_norm * normed_h, axis=-1, keepdims=True)
        )
    ).astype(jnp.bfloat16)
    block = doubling_sum(doubling_sum(block, "sec", jnp.bfloat16), "dp", jnp.bfloat16)
    grad_w_out = block[:rows_dev]
    group_first = (lax.axis_index("sec") * n_dp + lax.axis_index("dp")) * ways * clips_dev
    all_rewards = block[rows_dev:].reshape(extra * cols)
    rewards_out = lax.dynamic_slice_in_dim(all_rewards, group_first, ways * clips_dev)
    return (rewards_out, grad_w_out, grad_hidden)


def solution(mesh):
    placed = (
        P(("sec", "dp", "seq"), None, None),
        P(("sec", "dp", "seq"), None),
        P(("sec", "dp", "seq"), None),
        P(("sec", "dp", "seq"), None, None),
        P(("sec", "dp", "seq")),
        P(),
        P(),
        P(),
        P(None, None, "seq"),
        P("seq", None),
        P("seq", None),
        P(),
        P(("sec", "dp")),
        P(("sec", "dp")),
    )
    return jax.shard_map(
        local,
        mesh=mesh,
        in_specs=placed,
        out_specs=(P(("sec", "dp")), P("seq", None), P(("sec", "dp", "seq"), None, None)),
        check_vma=False,
    )
```

```python
import jax
import jax.numpy as jnp
from jax import lax
from jax.sharding import PartitionSpec as P

D_REW = 2048
HEADS = 16
PROMPTS = 32


normalizing_sharpness = 10.0
epsilon = 1e-06
highest = lax.Precision.HIGHEST


def rotate(angle, first, second):
    cosine = jnp.cos(angle)
    sine_term = jnp.sin(angle)
    return (cosine * first + sine_term * second, cosine * second - sine_term * first)


def suffix(values):
    return jnp.sum(values, axis=1, keepdims=True) - jnp.cumsum(values, axis=1)


def local_path(motion):
    spin = motion[..., 0]
    theta = jnp.cumsum(spin, axis=1) - spin
    step_east, step_north = rotate(theta, motion[..., 1], motion[..., 2])
    path_east = jnp.cumsum(step_east, axis=1) - step_east
    path_north = jnp.cumsum(step_north, axis=1) - step_north
    return (theta, path_east, path_north)


def embed(motion, root_east, root_north, w_embed, root_rows):
    emb = jnp.einsum(
        "cfe,ed->cfd", motion.astype(jnp.bfloat16), w_embed, preferred_element_type=jnp.float32
    )
    emb = emb + root_east[..., None] * root_rows[0] + root_north[..., None] * root_rows[1]
    scale_rms = jnp.sqrt(jnp.mean(emb * emb, axis=-1, keepdims=True) + epsilon)
    return (emb / scale_rms, scale_rms)


def unit_rows(vectors):
    length = jnp.sqrt(jnp.sum(vectors * vectors, axis=-1, keepdims=True) + epsilon)
    return (vectors / length, length)


def bf16_parts(values):
    high = lax.reduce_precision(values, exponent_bits=8, mantissa_bits=7)
    rest = values - high
    middle = lax.reduce_precision(rest, exponent_bits=8, mantissa_bits=7)
    return jnp.stack([high, middle, rest - middle]).astype(jnp.bfloat16)


def norm_grad(grad, normed, scale_rms):
    return (grad - normed * jnp.mean(grad * normed, axis=-1, keepdims=True)) / scale_rms


def motion_grad(d_emb, normed_e, scale_rms, motion, theta, w_embed, root_rows):
    d_unemb = norm_grad(d_emb, normed_e, scale_rms)
    d_embedded = jnp.sum(
        jnp.einsum("pcfd,ed->pcfe", bf16_parts(d_unemb), w_embed, preferred_element_type=jnp.float32),
        axis=0,
    )
    grad_east = suffix(jnp.sum(d_unemb * root_rows[0], axis=-1))
    grad_north = suffix(jnp.sum(d_unemb * root_rows[1], axis=-1))
    vel_east = motion[..., 1]
    vel_north = motion[..., 2]
    d_east, d_north = rotate(-theta, grad_east, grad_north)
    cosine = jnp.cos(theta)
    sine_term = jnp.sin(theta)
    d_theta = grad_east * (cosine * vel_north - sine_term * vel_east) - grad_north * (
        cosine * vel_east + sine_term * vel_north
    )
    d_spin = suffix(d_theta)
    return d_embedded.at[..., 0].add(d_spin).at[..., 1].add(d_east).at[..., 2].add(d_north)


def xor_pairs(size, bit):
    return [(i, i ^ bit) for i in range(size)]


def halving_sum(chunks, axis, wire_types, ride=None):
    size = lax.axis_size(axis)
    me = lax.axis_index(axis)
    bits = size.bit_length() - 1
    assert 1 << bits == size
    buf = chunks.reshape((2,) * bits + chunks.shape[1:])
    for k in range(bits):
        mine = (me >> k) & 1
        keep = lax.dynamic_index_in_dim(buf, mine, axis=bits - 1 - k, keepdims=False)
        send = lax.dynamic_index_in_dim(buf, 1 - mine, axis=bits - 1 - k, keepdims=False)
        got = lax.ppermute(send.astype(wire_types[k]), axis, xor_pairs(size, 1 << k))
        buf = keep + got.astype(keep.dtype)
        if k == 0:
            buf, ride = lax.optimization_barrier((buf, ride))
    return buf, ride


def doubling_sum(value, axis, wire_type=None):
    size = lax.axis_size(axis)
    bits = size.bit_length() - 1
    assert 1 << bits == size
    for k in range(bits):
        if wire_type is None:
            value = value + lax.ppermute(value, axis, xor_pairs(size, 1 << k))
        else:
            sent = value.astype(wire_type)
            got = lax.ppermute(sent, axis, xor_pairs(size, 1 << k))
            value = sent.astype(value.dtype) + got.astype(value.dtype)
    return value


def local(
    hidden,
    cond_shift,
    cond_scale,
    noisy,
    noise_level,
    w_out,
    w_embed,
    w_root,
    w_qkv,
    w_proj,
    text_table,
    text_ids,
    prompt_index,
    reward_weight,
):
    clips_dev = hidden.shape[0]
    ways = lax.axis_size("seq")
    me = lax.axis_index("seq")
    head_size = D_REW // HEADS
    root_rows = w_root.astype(jnp.float32)

    vocab_rows = text_table.shape[0]
    local_ids = text_ids - me * vocab_rows
    inside = (local_ids >= 0) & (local_ids < vocab_rows)
    picked = jnp.take(text_table, jnp.clip(local_ids, 0, vocab_rows - 1), axis=0).astype(
        jnp.float32
    )
    text_part = jnp.sum(jnp.where(inside[..., None], picked, 0.0), axis=1)
    text_raw = doubling_sum(text_part, "seq")
    w_all = lax.all_gather(w_qkv, "seq", axis=0)

    hidden_f = hidden.astype(jnp.float32)
    centred = hidden_f - jnp.mean(hidden_f, axis=-1, keepdims=True)
    inv_std = lax.rsqrt(jnp.mean(centred * centred, axis=-1, keepdims=True) + epsilon)
    normed_h = centred * inv_std
    gain = 1.0 + cond_scale.astype(jnp.float32)[:, None, :]
    modulated = (normed_h * gain + cond_shift.astype(jnp.float32)[:, None, :]).astype(jnp.bfloat16)
    eps_pred = jnp.einsum("cfd,de->cfe", modulated, w_out, preferred_element_type=jnp.float32)
    level = noise_level[:, None, None]
    x_clean = noisy.astype(jnp.float32) - level * eps_pred
    theta, path_east, path_north = local_path(x_clean)
    normed_e, scale_rms = embed(x_clean, path_east, path_north, w_embed, root_rows)
    w_all, proj_send, emb_b, text_raw, modulated_t = lax.optimization_barrier(
        (w_all, w_proj, normed_e.astype(jnp.bfloat16), text_raw, jnp.swapaxes(modulated, 1, 2))
    )
    text_unit, text_len = unit_rows(text_raw)
    proj_b = lax.all_gather(proj_send, "seq", axis=0, tiled=True)
    projected = jnp.einsum(
        "cfd,hjdk->cfhjk",
        emb_b,
        w_all,
        preferred_element_type=jnp.float32,
    )
    query_unit, query_len = unit_rows(projected[:, :, :, 0])
    key_unit, key_len = unit_rows(projected[:, :, :, 1])
    asking_vectors_group = query_unit.astype(jnp.bfloat16)
    lookup_vectors_group = key_unit.astype(jnp.bfloat16)
    value_b = projected[:, :, :, 2].astype(jnp.bfloat16)
    similarity_table = normalizing_sharpness * jnp.einsum(
        "cfhd,cghd->chfg",
        asking_vectors_group,
        lookup_vectors_group,
        preferred_element_type=jnp.float32,
    )
    expo = jnp.exp(similarity_table)
    focus_probabilities = expo / jnp.sum(expo, axis=-1, keepdims=True)
    attention_b = focus_probabilities.astype(jnp.bfloat16)
    column_mass = jnp.sum(attention_b, axis=2, dtype=jnp.float32)
    value_f = value_b.astype(jnp.float32)
    pooled = jnp.einsum("chg,cghd->chd", column_mass, value_f, precision=highest)
    pooled_b = pooled.astype(jnp.bfloat16).reshape(clips_dev, D_REW)
    motion_emb = jnp.dot(pooled_b, proj_b, preferred_element_type=jnp.float32)
    prompts = lax.dynamic_slice_in_dim(prompt_index, me * clips_dev, clips_dev)
    weights = lax.dynamic_slice_in_dim(reward_weight, me * clips_dev, clips_dev)
    choose = (prompts[:, None] == jnp.arange(PROMPTS)[None, :]).astype(jnp.float32)
    target = jnp.dot(choose, text_unit, precision=highest)
    emb_len = jnp.sqrt(jnp.sum(motion_emb * motion_emb, axis=-1) + epsilon)
    rewards = jnp.sum(motion_emb * target, axis=-1) / emb_len
    d_memb = (
        (-weights)[:, None]
        * (target - rewards[:, None] * motion_emb / emb_len[:, None])
        / emb_len[:, None]
    )
    d_pooled = jnp.sum(
        jnp.einsum("pcn,rn->pcr", bf16_parts(d_memb), proj_b, preferred_element_type=jnp.float32),
        axis=0,
    ).reshape(clips_dev, HEADS, head_size)
    reduction_dimension = jnp.einsum("chd,cghd->chg", d_pooled, value_f, precision=highest)
    d_value = jnp.transpose(column_mass, (0, 2, 1))[..., None] * d_pooled[:, None]
    pairwise_dot_similarity = jnp.sum(
        focus_probabilities * reduction_dimension[:, :, None, :], axis=-1, keepdims=True
    )
    similarity_derivative = (
        normalizing_sharpness
        * focus_probabilities
        * (reduction_dimension[:, :, None, :] - pairwise_dot_similarity)
    ).astype(jnp.bfloat16)
    d_qu = jnp.einsum(
        "chfg,cghd->cfhd",
        similarity_derivative,
        lookup_vectors_group,
        preferred_element_type=jnp.float32,
    )
    d_ku = jnp.einsum(
        "chfg,cfhd->cghd",
        similarity_derivative,
        asking_vectors_group,
        preferred_element_type=jnp.float32,
    )
    d_query = (d_qu - query_unit * jnp.sum(query_unit * d_qu, axis=-1, keepdims=True)) / query_len
    d_key = (d_ku - key_unit * jnp.sum(key_unit * d_ku, axis=-1, keepdims=True)) / key_len
    d_proj = jnp.stack([d_query, d_key, d_value], axis=3).astype(jnp.bfloat16)
    d_emb = jnp.einsum("cfhjk,hjdk->cfd", d_proj, w_all, preferred_element_type=jnp.float32)
    d_motion = motion_grad(d_emb, normed_e, scale_rms, x_clean, theta, w_embed, root_rows)
    d_eps_b = (-level * d_motion).astype(jnp.bfloat16)
    grad_term = jnp.einsum(
        "cdf,cfe->de", modulated_t, d_eps_b, preferred_element_type=jnp.float32
    )

    rows_dev = w_out.shape[0] // ways
    cols = grad_term.shape[1]
    n_dp = lax.axis_size("dp")
    total_clips = clips_dev * ways * n_dp * lax.axis_size("sec")
    extra = -(-total_clips // cols)
    extra = -(-extra // 8) * 8
    first_clip = (
        (lax.axis_index("sec") * n_dp + lax.axis_index("dp")) * ways + me
    ) * clips_dev
    columns = jnp.arange(extra * cols)
    slots = columns[None, :] == (first_clip + jnp.arange(clips_dev))[:, None]
    reward_rows = jnp.sum(jnp.where(slots, rewards[:, None], 0.0), axis=0).reshape(extra, cols)
    stacked = jnp.concatenate(
        [
            grad_term.reshape(ways, rows_dev, cols),
            jnp.broadcast_to(reward_rows[None], (ways, extra, cols)),
        ],
        axis=1,
    )
    seq_bits = ways.bit_length() - 1
    block, d_eps_b = halving_sum(stacked, "seq", [jnp.bfloat16] * seq_bits, ride=d_eps_b)
    d_mod = jnp.einsum("cfe,de->cfd", d_eps_b, w_out, preferred_element_type=jnp.float32)
    d_norm = d_mod * gain
    grad_hidden = (
        inv_std
        * (
            d_norm
            - jnp.mean(d_norm, axis=-1, keepdims=True)
            - normed_h * jnp.mean(d_norm * normed_h, axis=-1, keepdims=True)
        )
    ).astype(jnp.bfloat16)
    block = doubling_sum(doubling_sum(block, "sec", jnp.bfloat16), "dp", jnp.bfloat16)
    grad_w_out = block[:rows_dev]
    group_first = (lax.axis_index("sec") * n_dp + lax.axis_index("dp")) * ways * clips_dev
    all_rewards = block[rows_dev:].reshape(extra * cols)
    rewards_out = lax.dynamic_slice_in_dim(all_rewards, group_first, ways * clips_dev)
    return (rewards_out, grad_w_out, grad_hidden)


def solution(mesh):
    placed = (
        P(("sec", "dp", "seq"), None, None),
        P(("sec", "dp", "seq"), None),
        P(("sec", "dp", "seq"), None),
        P(("sec", "dp", "seq"), None, None),
        P(("sec", "dp", "seq")),
        P(),
        P(),
        P(),
        P(None, None, "seq"),
        P("seq", None),
        P("seq", None),
        P(),
        P(("sec", "dp")),
        P(("sec", "dp")),
    )
    return jax.shard_map(
        local,
        mesh=mesh,
        in_specs=placed,
        out_specs=(P(("sec", "dp")), P("seq", None), P(("sec", "dp", "seq"), None, None)),
        check_vma=False,
    )
```

```python
import jax
import jax.numpy as jnp
from jax import lax
from jax.sharding import PartitionSpec as P

D_REW = 2048
HEADS = 16
PROMPTS = 32


normalizing_sharpness = 10.0
epsilon = 1e-06
highest = lax.Precision.HIGHEST


def rotate(angle, first, second):
    cosine = jnp.cos(angle)
    sine_term = jnp.sin(angle)
    return (cosine * first + sine_term * second, cosine * second - sine_term * first)


def suffix(values):
    return jnp.sum(values, axis=1, keepdims=True) - jnp.cumsum(values, axis=1)


def local_path(motion):
    spin = motion[..., 0]
    theta = jnp.cumsum(spin, axis=1) - spin
    step_east, step_north = rotate(theta, motion[..., 1], motion[..., 2])
    path_east = jnp.cumsum(step_east, axis=1) - step_east
    path_north = jnp.cumsum(step_north, axis=1) - step_north
    return (theta, path_east, path_north)


def embed(motion, root_east, root_north, w_embed, root_rows):
    emb = jnp.einsum(
        "cfe,ed->cfd", motion.astype(jnp.bfloat16), w_embed, preferred_element_type=jnp.float32
    )
    emb = emb + root_east[..., None] * root_rows[0] + root_north[..., None] * root_rows[1]
    scale_rms = jnp.sqrt(jnp.mean(emb * emb, axis=-1, keepdims=True) + epsilon)
    return (emb / scale_rms, scale_rms)


def unit_rows(vectors):
    length = jnp.sqrt(jnp.sum(vectors * vectors, axis=-1, keepdims=True) + epsilon)
    return (vectors / length, length)


def bf16_parts(values):
    high = lax.reduce_precision(values, exponent_bits=8, mantissa_bits=7)
    rest = values - high
    middle = lax.reduce_precision(rest, exponent_bits=8, mantissa_bits=7)
    return jnp.stack([high, middle, rest - middle]).astype(jnp.bfloat16)


def norm_grad(grad, normed, scale_rms):
    return (grad - normed * jnp.mean(grad * normed, axis=-1, keepdims=True)) / scale_rms


def motion_grad(d_emb, normed_e, scale_rms, motion, theta, w_embed, root_rows):
    d_unemb = norm_grad(d_emb, normed_e, scale_rms)
    d_embedded = jnp.sum(
        jnp.einsum("pcfd,ed->pcfe", bf16_parts(d_unemb), w_embed, preferred_element_type=jnp.float32),
        axis=0,
    )
    grad_east = suffix(jnp.sum(d_unemb * root_rows[0], axis=-1))
    grad_north = suffix(jnp.sum(d_unemb * root_rows[1], axis=-1))
    vel_east = motion[..., 1]
    vel_north = motion[..., 2]
    d_east, d_north = rotate(-theta, grad_east, grad_north)
    cosine = jnp.cos(theta)
    sine_term = jnp.sin(theta)
    d_theta = grad_east * (cosine * vel_north - sine_term * vel_east) - grad_north * (
        cosine * vel_east + sine_term * vel_north
    )
    d_spin = suffix(d_theta)
    return d_embedded.at[..., 0].add(d_spin).at[..., 1].add(d_east).at[..., 2].add(d_north)


def xor_pairs(size, bit):
    return [(i, i ^ bit) for i in range(size)]


def halving_sum(chunks, axis, wire_types, ride=None):
    size = lax.axis_size(axis)
    me = lax.axis_index(axis)
    bits = size.bit_length() - 1
    assert 1 << bits == size
    buf = chunks.reshape((2,) * bits + chunks.shape[1:])
    for k in range(bits):
        mine = (me >> k) & 1
        keep = lax.dynamic_index_in_dim(buf, mine, axis=bits - 1 - k, keepdims=False)
        send = lax.dynamic_index_in_dim(buf, 1 - mine, axis=bits - 1 - k, keepdims=False)
        got = lax.ppermute(send.astype(wire_types[k]), axis, xor_pairs(size, 1 << k))
        buf = keep + got.astype(keep.dtype)
        if k == 0:
            buf, ride = lax.optimization_barrier((buf, ride))
    return buf, ride


def doubling_sum(value, axis, wire_type=None):
    size = lax.axis_size(axis)
    bits = size.bit_length() - 1
    assert 1 << bits == size
    for k in range(bits):
        if wire_type is None:
            value = value + lax.ppermute(value, axis, xor_pairs(size, 1 << k))
        else:
            sent = value.astype(wire_type)
            got = lax.ppermute(sent, axis, xor_pairs(size, 1 << k))
            value = sent.astype(value.dtype) + got.astype(value.dtype)
    return value


def local(
    hidden,
    cond_shift,
    cond_scale,
    noisy,
    noise_level,
    w_out,
    w_embed,
    w_root,
    w_qkv,
    w_proj,
    text_table,
    text_ids,
    prompt_index,
    reward_weight,
):
    clips_dev = hidden.shape[0]
    ways = lax.axis_size("seq")
    me = lax.axis_index("seq")
    head_size = D_REW // HEADS
    root_rows = w_root.astype(jnp.float32)

    vocab_rows = text_table.shape[0]
    local_ids = text_ids - me * vocab_rows
    inside = (local_ids >= 0) & (local_ids < vocab_rows)
    picked = jnp.take(text_table, jnp.clip(local_ids, 0, vocab_rows - 1), axis=0).astype(
        jnp.float32
    )
    text_part = jnp.sum(jnp.where(inside[..., None], picked, 0.0), axis=1)
    text_raw = doubling_sum(text_part, "seq")
    w_all = lax.all_gather(w_qkv, "seq", axis=0)

    hidden_f = hidden.astype(jnp.float32)
    centred = hidden_f - jnp.mean(hidden_f, axis=-1, keepdims=True)
    inv_std = lax.rsqrt(jnp.mean(centred * centred, axis=-1, keepdims=True) + epsilon)
    normed_h = centred * inv_std
    gain = 1.0 + cond_scale.astype(jnp.float32)[:, None, :]
    modulated = (normed_h * gain + cond_shift.astype(jnp.float32)[:, None, :]).astype(jnp.bfloat16)
    eps_pred = jnp.einsum("cfd,de->cfe", modulated, w_out, preferred_element_type=jnp.float32)
    level = noise_level[:, None, None]
    x_clean = noisy.astype(jnp.float32) - level * eps_pred
    theta, path_east, path_north = local_path(x_clean)
    normed_e, scale_rms = embed(x_clean, path_east, path_north, w_embed, root_rows)
    w_all, proj_send, emb_b, text_raw, modulated_t = lax.optimization_barrier(
        (w_all, w_proj, normed_e.astype(jnp.bfloat16), text_raw, jnp.swapaxes(modulated, 1, 2))
    )
    text_unit, text_len = unit_rows(text_raw)
    proj_b = lax.all_gather(proj_send, "seq", axis=0, tiled=True)
    projected = jnp.einsum(
        "cfd,hjdk->cfhjk",
        emb_b,
        w_all,
        preferred_element_type=jnp.float32,
    )
    query_unit, query_len = unit_rows(projected[:, :, :, 0])
    key_unit, key_len = unit_rows(projected[:, :, :, 1])
    asking_vectors_group = query_unit.astype(jnp.bfloat16)
    lookup_vectors_group = key_unit.astype(jnp.bfloat16)
    value_b = projected[:, :, :, 2].astype(jnp.bfloat16)
    similarity_table = normalizing_sharpness * jnp.einsum(
        "cfhd,cghd->chfg",
        asking_vectors_group,
        lookup_vectors_group,
        preferred_element_type=jnp.float32,
    )
    expo = jnp.exp(similarity_table)
    focus_probabilities = expo / jnp.sum(expo, axis=-1, keepdims=True)
    attention_b = focus_probabilities.astype(jnp.bfloat16)
    column_mass = jnp.sum(attention_b, axis=2, dtype=jnp.float32)
    value_f = value_b.astype(jnp.float32)
    pooled = jnp.sum(
        jnp.einsum(
            "pchg,cghd->pchd", bf16_parts(column_mass), value_b, preferred_element_type=jnp.float32
        ),
        axis=0,
    )
    pooled_b = pooled.astype(jnp.bfloat16).reshape(clips_dev, D_REW)
    motion_emb = jnp.dot(pooled_b, proj_b, preferred_element_type=jnp.float32)
    prompts = lax.dynamic_slice_in_dim(prompt_index, me * clips_dev, clips_dev)
    weights = lax.dynamic_slice_in_dim(reward_weight, me * clips_dev, clips_dev)
    choose = (prompts[:, None] == jnp.arange(PROMPTS)[None, :]).astype(jnp.float32)
    target = jnp.dot(choose, text_unit, precision=highest)
    emb_len = jnp.sqrt(jnp.sum(motion_emb * motion_emb, axis=-1) + epsilon)
    rewards = jnp.sum(motion_emb * target, axis=-1) / emb_len
    d_memb = (
        (-weights)[:, None]
        * (target - rewards[:, None] * motion_emb / emb_len[:, None])
        / emb_len[:, None]
    )
    d_pooled = jnp.sum(
        jnp.einsum("pcn,rn->pcr", bf16_parts(d_memb), proj_b, preferred_element_type=jnp.float32),
        axis=0,
    ).reshape(clips_dev, HEADS, head_size)
    reduction_dimension = jnp.sum(
        jnp.einsum(
            "pchd,cghd->pchg", bf16_parts(d_pooled), value_b, preferred_element_type=jnp.float32
        ),
        axis=0,
    )
    d_value = jnp.transpose(column_mass, (0, 2, 1))[..., None] * d_pooled[:, None]
    pairwise_dot_similarity = jnp.sum(
        focus_probabilities * reduction_dimension[:, :, None, :], axis=-1, keepdims=True
    )
    similarity_derivative = (
        normalizing_sharpness
        * focus_probabilities
        * (reduction_dimension[:, :, None, :] - pairwise_dot_similarity)
    ).astype(jnp.bfloat16)
    d_qu = jnp.einsum(
        "chfg,cghd->cfhd",
        similarity_derivative,
        lookup_vectors_group,
        preferred_element_type=jnp.float32,
    )
    d_ku = jnp.einsum(
        "chfg,cfhd->cghd",
        similarity_derivative,
        asking_vectors_group,
        preferred_element_type=jnp.float32,
    )
    d_query = (d_qu - query_unit * jnp.sum(query_unit * d_qu, axis=-1, keepdims=True)) / query_len
    d_key = (d_ku - key_unit * jnp.sum(key_unit * d_ku, axis=-1, keepdims=True)) / key_len
    d_proj = jnp.stack([d_query, d_key, d_value], axis=3).astype(jnp.bfloat16)
    d_emb = jnp.einsum("cfhjk,hjdk->cfd", d_proj, w_all, preferred_element_type=jnp.float32)
    d_motion = motion_grad(d_emb, normed_e, scale_rms, x_clean, theta, w_embed, root_rows)
    d_eps_b = (-level * d_motion).astype(jnp.bfloat16)
    grad_term = jnp.einsum(
        "cdf,cfe->de", modulated_t, d_eps_b, preferred_element_type=jnp.float32
    )

    rows_dev = w_out.shape[0] // ways
    cols = grad_term.shape[1]
    n_dp = lax.axis_size("dp")
    total_clips = clips_dev * ways * n_dp * lax.axis_size("sec")
    extra = -(-total_clips // cols)
    extra = -(-extra // 8) * 8
    first_clip = (
        (lax.axis_index("sec") * n_dp + lax.axis_index("dp")) * ways + me
    ) * clips_dev
    columns = jnp.arange(extra * cols)
    slots = columns[None, :] == (first_clip + jnp.arange(clips_dev))[:, None]
    reward_rows = jnp.sum(jnp.where(slots, rewards[:, None], 0.0), axis=0).reshape(extra, cols)
    stacked = jnp.concatenate(
        [
            grad_term.reshape(ways, rows_dev, cols),
            jnp.broadcast_to(reward_rows[None], (ways, extra, cols)),
        ],
        axis=1,
    )
    seq_bits = ways.bit_length() - 1
    block, d_eps_b = halving_sum(stacked, "seq", [jnp.bfloat16] * seq_bits, ride=d_eps_b)
    d_mod = jnp.einsum("cfe,de->cfd", d_eps_b, w_out, preferred_element_type=jnp.float32)
    d_norm = d_mod * gain
    grad_hidden = (
        inv_std
        * (
            d_norm
            - jnp.mean(d_norm, axis=-1, keepdims=True)
            - normed_h * jnp.mean(d_norm * normed_h, axis=-1, keepdims=True)
        )
    ).astype(jnp.bfloat16)
    block = doubling_sum(doubling_sum(block, "sec", jnp.bfloat16), "dp", jnp.bfloat16)
    grad_w_out = block[:rows_dev]
    group_first = (lax.axis_index("sec") * n_dp + lax.axis_index("dp")) * ways * clips_dev
    all_rewards = block[rows_dev:].reshape(extra * cols)
    rewards_out = lax.dynamic_slice_in_dim(all_rewards, group_first, ways * clips_dev)
    return (rewards_out, grad_w_out, grad_hidden)


def solution(mesh):
    placed = (
        P(("sec", "dp", "seq"), None, None),
        P(("sec", "dp", "seq"), None),
        P(("sec", "dp", "seq"), None),
        P(("sec", "dp", "seq"), None, None),
        P(("sec", "dp", "seq")),
        P(),
        P(),
        P(),
        P(None, None, "seq"),
        P("seq", None),
        P("seq", None),
        P(),
        P(("sec", "dp")),
        P(("sec", "dp")),
    )
    return jax.shard_map(
        local,
        mesh=mesh,
        in_specs=placed,
        out_specs=(P(("sec", "dp")), P("seq", None), P(("sec", "dp", "seq"), None, None)),
        check_vma=False,
    )
```
